32 devices in a mesh: ctx: 8 (over z, y), tp: 4 (over x, core).
Axes of the slice: x: 2, y: 2, z: 4, core: 2. Of those that a mesh axis runs over, the one named last changes fastest.
Arguments:
- queries: bfloat16 [2048, 16, 128], P('ctx', 'tp'), may hold values from -12 to 12
- keys: bfloat16 [2048, 8, 128], P('ctx', 'tp'), may hold values from -6 to 6
- values: bfloat16 [2048, 8, 128], P('ctx', 'tp'), may hold values from -6 to 6
- residual: bfloat16 [2048, 3072], P('ctx', 'tp'), may hold values from -6 to 6
- out_weight: bfloat16 [16, 128, 3072], P(None, None, 'tp'), may hold values from -1 to 1
- post_gain: bfloat16 [3072], P('tp'), may hold values from 0.099609375 to 1.8984375
Outputs:
- mixed: bfloat16 [2048, 3072], P('ctx', 'tp')
The draws below stay inside these ranges and needn't reach their ends.
All inputs are finite; a program needn't handle non-finite values.
Results may differ from the reference program's by a relative error of at most 0.015.
Values may be sent and summed in bfloat16 or wider, within the bound.
No kernel may reach another device: no remote copies, remote signals or barrier semaphores. Data moves between devices by JAX's collectives and lax.ppermute only.
A program may use at most 64 MiB of HBM per device.

```python
import jax
import jax.numpy as jnp
from jax import lax

TOK_DEV = 256
WINDOW_TOKENS = 4096
QUERY_HEADS = 16
KEY_VALUE_HEADS = 8
HEAD_WIDTH = 128
D = 3072
SEQUENCE_TOKENS = 2048


def draw_out_weight(key, part):
    columns = jnp.arange(D, dtype=jnp.float32) / D
    rising = 10.0 ** columns / 10.0
    base = jax.random.uniform(key, (QUERY_HEADS, HEAD_WIDTH, D), jnp.float32, -1.0, 1.0)
    return (base * rising).astype(jnp.bfloat16)


def level_of(stream_key, shape, pieces, smallest, largest):
    gain = 1.0
    for axis_at, blocks in pieces:
        heights = jax.random.uniform(jax.random.fold_in(jax.random.fold_in(stream_key, 6), axis_at), (blocks,), jnp.float32, smallest / len(pieces), largest / len(pieces))
        gain = gain * jnp.repeat(jnp.exp(heights), shape[axis_at] // blocks).reshape((-1,) + (1,) * (len(shape) - 1 - axis_at))
    return gain


def bell_draw(stream_key, extent, width, limit, pieces=(), kind=jnp.bfloat16):
    entries = jax.random.normal(stream_key, extent, jnp.float32) * width
    if len(pieces) > 0:
        entries = level_of(stream_key, extent, pieces, -0.22, 0.18) * entries
    return jnp.clip(entries, min=-limit, max=limit).astype(kind)


def setup_inputs(seed: int = 0) -> dict:
    splits = jax.random.split(jax.random.key(seed), 7)
    return {
        "queries": bell_draw(splits[0], (SEQUENCE_TOKENS, QUERY_HEADS, HEAD_WIDTH), 3.0, 12.0, ((0, 8), (1, 4))),
        "keys": bell_draw(splits[1], (SEQUENCE_TOKENS, KEY_VALUE_HEADS, HEAD_WIDTH), 1.0, 6.0, ((0, 8), (1, 4))),
        "values": bell_draw(splits[2], (SEQUENCE_TOKENS, KEY_VALUE_HEADS, HEAD_WIDTH), 1.0, 6.0, ((0, 8), (1, 4))),
        "residual": bell_draw(splits[3], (SEQUENCE_TOKENS, D), 1.0, 6.0, ((0, 8), (1, 4))),
        "out_weight": draw_out_weight(jax.random.fold_in(splits[6], 71), 0),
        "post_gain": jnp.clip(1.0 + 0.18 * jax.random.normal(splits[5], (D,), jnp.float32), 0.099609375, 1.8984375).astype(jnp.bfloat16),
    }


softcap_value = 50.0
query_scale = 1.0 / 12.0
rope_base = 10000.0

def rotate(values_in, positions):
    half_width = values_in.shape[-1] // 2
    steps_half = jnp.arange(half_width, dtype=jnp.float32)
    inverse = rope_base ** (-2.0 * steps_half / values_in.shape[-1])
    angles = positions.astype(jnp.float32)[..., None] * inverse
    cosine = jnp.cos(angles)
    sine_part = jnp.sin(angles)
    first_half = values_in[..., :half_width]
    second_half = values_in[..., half_width:]
    return jnp.concatenate([first_half * cosine - second_half * sine_part, second_half * cosine + first_half * sine_part], axis=-1)

def reference(queries, keys, values, residual, out_weight, post_gain):
    token_length = SEQUENCE_TOKENS
    heads_per_group = QUERY_HEADS // KEY_VALUE_HEADS
    positions = jnp.arange(token_length, dtype=jnp.int32)[:, None]
    rotary_queries = rotate(queries.astype(jnp.float32), positions).astype(jnp.bfloat16)
    rotary_queries = lax.optimization_barrier(rotary_queries)
    rotary_keys = rotate(keys.astype(jnp.float32), positions).astype(jnp.bfloat16)
    rotary_keys = lax.optimization_barrier(rotary_keys)
    grouped_query = rotary_queries.reshape(token_length, KEY_VALUE_HEADS, heads_per_group, HEAD_WIDTH)
    padded_keys = jnp.concatenate([jnp.zeros((WINDOW_TOKENS, KEY_VALUE_HEADS, HEAD_WIDTH), jnp.bfloat16), rotary_keys], axis=0)
    padded_values = jnp.concatenate([jnp.zeros((WINDOW_TOKENS, KEY_VALUE_HEADS, HEAD_WIDTH), jnp.bfloat16), values], axis=0)
    block_rows = TOK_DEV

    def attend(block_index):
        begin = block_index * block_rows
        query_block = lax.dynamic_slice_in_dim(grouped_query, begin, block_rows, 0)
        key_block = lax.dynamic_slice_in_dim(padded_keys, begin, WINDOW_TOKENS + block_rows, 0)
        value_block = lax.dynamic_slice_in_dim(padded_values, begin, WINDOW_TOKENS + block_rows, 0)
        scores = jnp.einsum('qgrh,kgh->grqk', query_block.astype(jnp.float32), key_block.astype(jnp.float32)) * query_scale
        capped = softcap_value * jnp.tanh(scores / softcap_value)
        query_pos = begin + jnp.arange(block_rows, dtype=jnp.int32)
        key_pos = begin - WINDOW_TOKENS + jnp.arange(WINDOW_TOKENS + block_rows, dtype=jnp.int32)
        distance = query_pos[:, None] - key_pos[None, :]
        allowed = (distance >= 0) & (distance < WINDOW_TOKENS) & (key_pos[None, :] >= 0)
        weights = jnp.where(allowed, jnp.exp(capped), 0.0)
        denominator = lax.optimization_barrier(jnp.sum(weights, axis=-1))
        rounded = lax.optimization_barrier(weights.astype(jnp.bfloat16))
        numerator = jnp.einsum('grqk,kgh->grqh', rounded.astype(jnp.float32), value_block.astype(jnp.float32))
        attended = (numerator / denominator[..., None]).astype(jnp.bfloat16)
        return jnp.transpose(attended, (2, 0, 1, 3)).reshape(block_rows, QUERY_HEADS * HEAD_WIDTH)
    heads_out = lax.map(attend, jnp.arange(token_length // block_rows, dtype=jnp.int32)).reshape(token_length, QUERY_HEADS * HEAD_WIDTH)
    projected = jnp.dot(heads_out, out_weight.reshape(QUERY_HEADS * HEAD_WIDTH, D), preferred_element_type=jnp.float32)
    mean_square = lax.optimization_barrier(jnp.sum(projected * projected, axis=1)) / D
    normed = projected * lax.rsqrt(mean_square + 1e-06)[:, None] * post_gain.astype(jnp.float32)
    mixed = residual.astype(jnp.float32) + normed
    return mixed.astype(jnp.bfloat16)
```

```python
import jax
import jax.numpy as jnp
from jax import lax
from jax.sharding import PartitionSpec as P

WINDOW_TOKENS = 4096
D = 3072


softcap_value = 50.0
query_scale = 1.0 / 12.0
rope_base = 10000.0


def passed_along(value, axis, steps):
    count = lax.axis_size(axis)
    first, last = (max(0, -steps), min(count, count - steps))
    return lax.ppermute(value, axis, [(source, source + steps) for source in range(first, last)])


def rotate(values_in, positions):
    half_width = values_in.shape[-1] // 2
    steps_half = jnp.arange(half_width, dtype=jnp.float32)
    inverse = rope_base ** (-2.0 * steps_half / values_in.shape[-1])
    angles = positions.astype(jnp.float32)[..., None] * inverse
    cosine = jnp.cos(angles)
    sine_part = jnp.sin(angles)
    first_half = values_in[..., :half_width]
    second_half = values_in[..., half_width:]
    return jnp.concatenate(
        [
            first_half * cosine - second_half * sine_part,
            second_half * cosine + first_half * sine_part,
        ],
        axis=-1,
    )


def attend_keys(state, key_block, value_block, query_pos, key_pos, rotary_queries, extra=None):
    numerators, denominators = state
    scores = (
        jnp.einsum("sgrh,kgh->grsk", rotary_queries, key_block, preferred_element_type=jnp.float32)
        * query_scale
    )
    capped = softcap_value * jnp.tanh(scores / softcap_value)
    distance = query_pos[:, None] - key_pos[None, :]
    allowed = (distance >= 0) & (distance < WINDOW_TOKENS) & (key_pos[None, :] >= 0)
    if extra is not None:
        allowed = allowed & extra
    weights = jnp.where(allowed[None, None], jnp.exp(capped), 0.0)
    denominators = denominators + jnp.sum(weights, axis=-1)
    numerators = numerators + jnp.einsum(
        "grsk,kgh->grsh",
        weights.astype(jnp.bfloat16),
        value_block,
        preferred_element_type=jnp.float32,
    )
    return (numerators, denominators)


def local(queries, keys, values, residual, out_weight, post_gain):
    rows = queries.shape[0]
    q_heads = queries.shape[1]
    head_size = queries.shape[2]
    kv_heads = keys.shape[1]
    heads_per_group = q_heads // kv_heads
    cycle_size = lax.axis_size("ctx")
    device_index = lax.axis_index("ctx")
    reach = min((WINDOW_TOKENS + rows - 2) // rows, cycle_size - 1)
    offsets = jnp.arange(rows, dtype=jnp.int32)
    query_pos = device_index * rows + offsets
    gather_all = reach == cycle_size - 1
    if gather_all and reach > 0:
        stacked = jnp.concatenate([keys, values], axis=1)
        gathered = lax.all_gather(stacked, "ctx", axis=0, tiled=True)
    positions = query_pos[:, None]
    rotary_queries = rotate(queries.astype(jnp.float32), positions).astype(jnp.bfloat16)
    rotary_queries = rotary_queries.reshape(rows, kv_heads, heads_per_group, head_size)
    rotary_keys = rotate(keys.astype(jnp.float32), positions).astype(jnp.bfloat16)
    state = (
        jnp.zeros((kv_heads, heads_per_group, rows, head_size), jnp.float32),
        jnp.zeros((kv_heads, heads_per_group, rows), jnp.float32),
    )
    state = attend_keys(state, rotary_keys, values, query_pos, query_pos, rotary_queries)
    if gather_all and reach > 0:
        earlier = reach * rows
        key_pos = jnp.arange(earlier, dtype=jnp.int32)
        far_keys = rotate(gathered[:earlier, :kv_heads].astype(jnp.float32), key_pos[:, None]).astype(jnp.bfloat16)
        far_values = gathered[:earlier, kv_heads:]
        before = (key_pos < device_index * rows)[None, :]
        state = attend_keys(state, far_keys, far_values, query_pos, key_pos, rotary_queries, before)
    elif reach > 0:

        def advance(step_index, carried):
            running, key_block, value_block = carried
            key_block, value_block = passed_along((key_block, value_block), "ctx", 1)
            key_pos = (device_index - step_index - 1) * rows + offsets
            running = attend_keys(running, key_block, value_block, query_pos, key_pos, rotary_queries)
            return (running, key_block, value_block)

        state, unused_keys, unused_values = lax.fori_loop(
            0, reach, advance, (state, rotary_keys, values)
        )
    numerators, denominators = state
    attended = (numerators / denominators[..., None]).astype(jnp.bfloat16)
    attended = jnp.transpose(attended, (2, 0, 1, 3)).reshape(rows, q_heads, head_size)
    local_cols = out_weight.shape[2]
    piece = lax.all_gather(attended, "tp", axis=1, tiled=True)
    heads_in = piece.shape[1]
    weight_rows = out_weight.reshape(heads_in * head_size, local_cols)
    projected = jnp.dot(
        piece.reshape(rows, heads_in * head_size), weight_rows, preferred_element_type=jnp.float32
    )
    square_sums = lax.psum(jnp.sum(projected * projected, axis=1), "tp")
    normed = projected * lax.rsqrt(square_sums / D + 1e-06)[:, None] * post_gain.astype(jnp.float32)
    mixed = residual.astype(jnp.float32) + normed
    return mixed.astype(jnp.bfloat16)


def solution(mesh):
    in_specs = (
        P("ctx", "tp", None),
        P("ctx", "tp", None),
        P("ctx", "tp", None),
        P("ctx", "tp"),
        P(None, None, "tp"),
        P("tp"),
    )
    out_specs = P("ctx", "tp")
    return jax.shard_map(local, mesh=mesh, in_specs=in_specs, out_specs=out_specs, check_vma=False)
```

```python
import jax
import jax.numpy as jnp
from jax import lax
from jax.sharding import PartitionSpec as P

WINDOW_TOKENS = 4096
D = 3072


softcap_value = 50.0
query_scale = 1.0 / 12.0
rope_base = 10000.0


def passed_along(value, axis, steps):
    count = lax.axis_size(axis)
    first, last = (max(0, -steps), min(count, count - steps))
    return lax.ppermute(value, axis, [(source, source + steps) for source in range(first, last)])


def rotate(values_in, positions):
    half_width = values_in.shape[-1] // 2
    steps_half = jnp.arange(half_width, dtype=jnp.float32)
    inverse = rope_base ** (-2.0 * steps_half / values_in.shape[-1])
    angles = positions.astype(jnp.float32)[..., None] * inverse
    cosine = jnp.cos(angles)
    sine_part = jnp.sin(angles)
    first_half = values_in[..., :half_width]
    second_half = values_in[..., half_width:]
    return jnp.concatenate(
        [
            first_half * cosine - second_half * sine_part,
            second_half * cosine + first_half * sine_part,
        ],
        axis=-1,
    )


def attend_block(state, key_block, value_block, source, rotary_queries, device_index):
    numerators, denominators = state
    rows = key_block.shape[0]
    scores = (
        jnp.einsum("sgrh,kgh->grsk", rotary_queries, key_block, preferred_element_type=jnp.float32)
        * query_scale
    )
    capped = softcap_value * jnp.tanh(scores / softcap_value)
    offsets = jnp.arange(rows, dtype=jnp.int32)
    query_pos = device_index * rows + offsets
    key_pos = source * rows + offsets
    distance = query_pos[:, None] - key_pos[None, :]
    allowed = (distance >= 0) & (distance < WINDOW_TOKENS) & (key_pos[None, :] >= 0)
    weights = jnp.where(allowed[None, None], jnp.exp(capped), 0.0)
    denominators = denominators + jnp.sum(weights, axis=-1)
    numerators = numerators + jnp.einsum(
        "grsk,kgh->grsh",
        weights.astype(jnp.bfloat16),
        value_block,
        preferred_element_type=jnp.float32,
    )
    return (numerators, denominators)


def along_lines(state, key_block, value_block, rotary_queries, device_index, cycle_size):
    kv_heads = key_block.shape[1]
    outer = cycle_size // 2
    forward = [(source, source + 2) for source in range(cycle_size - 2)]
    up = [(source, source + 1) for source in range(0, cycle_size, 2)]
    down = [(source + 1, source) for source in range(0, cycle_size, 2)]
    plane = device_index // 2
    side = device_index % 2

    def attend_stacked(state, stacked, source):
        return attend_block(
            state, stacked[:, :kv_heads], stacked[:, kv_heads:], source, rotary_queries, device_index
        )

    line = jnp.concatenate([key_block, value_block], axis=1)
    for step in range(1, outer + 1):
        if step < outer:
            arrived = lax.ppermute(line, "ctx", forward)
        crossed = lax.ppermute(line, "ctx", up if step == 1 else up + down)
        state = attend_stacked(state, crossed, 2 * (plane - step + 1) + 1 - side)
        if step < outer:
            state = attend_stacked(state, arrived, device_index - 2 * step)
            line = arrived
    return state


def local(queries, keys, values, residual, out_weight, post_gain):
    rows = queries.shape[0]
    q_heads = queries.shape[1]
    head_size = queries.shape[2]
    kv_heads = keys.shape[1]
    heads_per_group = q_heads // kv_heads
    cycle_size = lax.axis_size("ctx")
    device_index = lax.axis_index("ctx")
    positions = (device_index * rows + jnp.arange(rows, dtype=jnp.int32))[:, None]
    rotary_queries = rotate(queries.astype(jnp.float32), positions).astype(jnp.bfloat16)
    rotary_queries = rotary_queries.reshape(rows, kv_heads, heads_per_group, head_size)
    rotary_keys = rotate(keys.astype(jnp.float32), positions).astype(jnp.bfloat16)
    reach = min((WINDOW_TOKENS + rows - 2) // rows, cycle_size - 1)
    state = (
        jnp.zeros((kv_heads, heads_per_group, rows, head_size), jnp.float32),
        jnp.zeros((kv_heads, heads_per_group, rows), jnp.float32),
    )
    state = attend_block(state, rotary_keys, values, device_index, rotary_queries, device_index)
    if reach == cycle_size - 1 and cycle_size % 2 == 0:
        state = along_lines(state, rotary_keys, values, rotary_queries, device_index, cycle_size)
    elif reach > 0:

        def advance(step_index, carried):
            running, key_block, value_block = carried
            key_block, value_block = passed_along((key_block, value_block), "ctx", 1)
            running = attend_block(
                running,
                key_block,
                value_block,
                device_index - step_index - 1,
                rotary_queries,
                device_index,
            )
            return (running, key_block, value_block)

        state, unused_keys, unused_values = lax.fori_loop(
            0, reach, advance, (state, rotary_keys, values)
        )
    numerators, denominators = state
    attended = (numerators / denominators[..., None]).astype(jnp.bfloat16)
    attended = jnp.transpose(attended, (2, 0, 1, 3)).reshape(rows, q_heads, head_size)
    local_cols = out_weight.shape[2]
    piece = lax.all_gather(attended, "tp", axis=1, tiled=True)
    heads_in = piece.shape[1]
    weight_rows = out_weight.reshape(heads_in * head_size, local_cols)
    projected = jnp.dot(
        piece.reshape(rows, heads_in * head_size), weight_rows, preferred_element_type=jnp.float32
    )
    partial_sums = jnp.sum(projected * projected, axis=1)
    square_sums = jnp.sum(lax.all_gather(partial_sums, "tp", axis=0), axis=0)
    normed = projected * lax.rsqrt(square_sums / D + 1e-06)[:, None] * post_gain.astype(jnp.float32)
    mixed = residual.astype(jnp.float32) + normed
    return mixed.astype(jnp.bfloat16)


def solution(mesh):
    in_specs = (
        P("ctx", "tp", None),
        P("ctx", "tp", None),
        P("ctx", "tp", None),
        P("ctx", "tp"),
        P(None, None, "tp"),
        P("tp"),
    )
    out_specs = P("ctx", "tp")
    return jax.shard_map(local, mesh=mesh, in_specs=in_specs, out_specs=out_specs, check_vma=False)
```

```python
import jax
import jax.numpy as jnp
from jax import lax
from jax.sharding import PartitionSpec as P

WINDOW_TOKENS = 4096
D = 3072


softcap_value = 50.0
query_scale = 1.0 / 12.0
rope_base = 10000.0


def passed_along(value, axis, steps):
    count = lax.axis_size(axis)
    first, last = (max(0, -steps), min(count, count - steps))
    return lax.ppermute(value, axis, [(source, source + steps) for source in range(first, last)])


def rotate(values_in, positions):
    half_width = values_in.shape[-1] // 2
    steps_half = jnp.arange(half_width, dtype=jnp.float32)
    inverse = rope_base ** (-2.0 * steps_half / values_in.shape[-1])
    angles = positions.astype(jnp.float32)[..., None] * inverse
    cosine = jnp.cos(angles)
    sine_part = jnp.sin(angles)
    first_half = values_in[..., :half_width]
    second_half = values_in[..., half_width:]
    return jnp.concatenate(
        [
            first_half * cosine - second_half * sine_part,
            second_half * cosine + first_half * sine_part,
        ],
        axis=-1,
    )


def attend_block(state, key_block, value_block, source, rotary_queries, device_index):
    numerators, denominators = state
    rows = key_block.shape[0]
    scores = (
        jnp.einsum("sgrh,kgh->grsk", rotary_queries, key_block, preferred_element_type=jnp.float32)
        * query_scale
    )
    capped = softcap_value * jnp.tanh(scores / softcap_value)
    offsets = jnp.arange(rows, dtype=jnp.int32)
    query_pos = device_index * rows + offsets
    key_pos = source * rows + offsets
    distance = query_pos[:, None] - key_pos[None, :]
    allowed = (distance >= 0) & (distance < WINDOW_TOKENS) & (key_pos[None, :] >= 0)
    weights = jnp.where(allowed[None, None], jnp.exp(capped), 0.0)
    denominators = denominators + jnp.sum(weights, axis=-1)
    numerators = numerators + jnp.einsum(
        "grsk,kgh->grsh",
        weights.astype(jnp.bfloat16),
        value_block,
        preferred_element_type=jnp.float32,
    )
    return (numerators, denominators)


def along_lines(state, key_block, value_block, rotary_queries, device_index, cycle_size):
    kv_heads = key_block.shape[1]
    outer = cycle_size // 2
    forward = [(source, source + 2) for source in range(cycle_size - 2)]
    up = [(source, source + 1) for source in range(0, cycle_size, 2)]
    down = [(source + 1, source) for source in range(0, cycle_size, 2)]
    plane = device_index // 2
    side = device_index % 2

    def attend_stacked(state, stacked, source):
        return attend_block(
            state, stacked[:, :kv_heads], stacked[:, kv_heads:], source, rotary_queries, device_index
        )

    line = jnp.concatenate([key_block, value_block], axis=1)
    for step in range(1, outer + 1):
        if step < outer:
            arrived = lax.ppermute(line, "ctx", forward)
        crossed = lax.ppermute(line, "ctx", up if step == 1 else up + down)
        state = attend_stacked(state, crossed, 2 * (plane - step + 1) + 1 - side)
        if step < outer:
            state = attend_stacked(state, arrived, device_index - 2 * step)
            line = arrived
    return state


def exchanged(piece, count, index):
    bit = 1
    while bit < count:
        other = lax.ppermute(piece, "tp", [(source, source ^ bit) for source in range(count)])
        lower = (index & bit) == 0
        first = jnp.where(lower, piece, other)
        second = jnp.where(lower, other, piece)
        piece = jnp.concatenate([first, second], axis=1)
        bit *= 2
    return piece


def summed(partial, count):
    bit = 1
    while bit < count:
        partial = partial + lax.ppermute(partial, "tp", [(source, source ^ bit) for source in range(count)])
        bit *= 2
    return partial


def local(queries, keys, values, residual, out_weight, post_gain):
    rows = queries.shape[0]
    q_heads = queries.shape[1]
    head_size = queries.shape[2]
    kv_heads = keys.shape[1]
    heads_per_group = q_heads // kv_heads
    cycle_size = lax.axis_size("ctx")
    device_index = lax.axis_index("ctx")
    positions = (device_index * rows + jnp.arange(rows, dtype=jnp.int32))[:, None]
    rotary_queries = rotate(queries.astype(jnp.float32), positions).astype(jnp.bfloat16)
    rotary_queries = rotary_queries.reshape(rows, kv_heads, heads_per_group, head_size)
    rotary_keys = rotate(keys.astype(jnp.float32), positions).astype(jnp.bfloat16)
    reach = min((WINDOW_TOKENS + rows - 2) // rows, cycle_size - 1)
    state = (
        jnp.zeros((kv_heads, heads_per_group, rows, head_size), jnp.float32),
        jnp.zeros((kv_heads, heads_per_group, rows), jnp.float32),
    )
    state = attend_block(state, rotary_keys, values, device_index, rotary_queries, device_index)
    if reach == cycle_size - 1 and cycle_size % 2 == 0:
        state = along_lines(state, rotary_keys, values, rotary_queries, device_index, cycle_size)
    elif reach > 0:

        def advance(step_index, carried):
            running, key_block, value_block = carried
            key_block, value_block = passed_along((key_block, value_block), "ctx", 1)
            running = attend_block(
                running,
                key_block,
                value_block,
                device_index - step_index - 1,
                rotary_queries,
                device_index,
            )
            return (running, key_block, value_block)

        state, unused_keys, unused_values = lax.fori_loop(
            0, reach, advance, (state, rotary_keys, values)
        )
    numerators, denominators = state
    attended = (numerators / denominators[..., None]).astype(jnp.bfloat16)
    attended = jnp.transpose(attended, (2, 0, 1, 3)).reshape(rows, q_heads, head_size)
    local_cols = out_weight.shape[2]
    tp_size = lax.axis_size("tp")
    tp_index = lax.axis_index("tp")
    butterfly = tp_size & (tp_size - 1) == 0
    if butterfly:
        piece = exchanged(attended, tp_size, tp_index)
    else:
        piece = lax.all_gather(attended, "tp", axis=1, tiled=True)
    heads_in = piece.shape[1]
    weight_rows = out_weight.reshape(heads_in * head_size, local_cols)
    projected = jnp.dot(
        piece.reshape(rows, heads_in * head_size), weight_rows, preferred_element_type=jnp.float32
    )
    partial_sums = jnp.sum(projected * projected, axis=1)
    if butterfly:
        square_sums = summed(partial_sums, tp_size)
    else:
        square_sums = jnp.sum(lax.all_gather(partial_sums, "tp", axis=0), axis=0)
    normed = projected * lax.rsqrt(square_sums / D + 1e-06)[:, None] * post_gain.astype(jnp.float32)
    mixed = residual.astype(jnp.float32) + normed
    return mixed.astype(jnp.bfloat16)


def solution(mesh):
    in_specs = (
        P("ctx", "tp", None),
        P("ctx", "tp", None),
        P("ctx", "tp", None),
        P("ctx", "tp"),
        P(None, None, "tp"),
        P("tp"),
    )
    out_specs = P("ctx", "tp")
    return jax.shard_map(local, mesh=mesh, in_specs=in_specs, out_specs=out_specs, check_vma=False)
```

```python
import jax
import jax.numpy as jnp
from jax import lax
from jax.sharding import PartitionSpec as P

WINDOW_TOKENS = 4096
D = 3072


softcap_value = 50.0
query_scale = 1.0 / 12.0
rope_base = 10000.0


def passed_along(value, axis, steps):
    count = lax.axis_size(axis)
    first, last = (max(0, -steps), min(count, count - steps))
    return lax.ppermute(value, axis, [(source, source + steps) for source in range(first, last)])


def rotate(values_in, positions):
    half_width = values_in.shape[-1] // 2
    steps_half = jnp.arange(half_width, dtype=jnp.float32)
    inverse = rope_base ** (-2.0 * steps_half / values_in.shape[-1])
    angles = positions.astype(jnp.float32)[..., None] * inverse
    cosine = jnp.cos(angles)
    sine_part = jnp.sin(angles)
    first_half = values_in[..., :half_width]
    second_half = values_in[..., half_width:]
    return jnp.concatenate(
        [
            first_half * cosine - second_half * sine_part,
            second_half * cosine + first_half * sine_part,
        ],
        axis=-1,
    )


def attend_block(state, key_block, value_block, source, rotary_queries, device_index):
    numerators, denominators = state
    rows = key_block.shape[0]
    scores = (
        jnp.einsum("sgrh,kgh->grsk", rotary_queries, key_block, preferred_element_type=jnp.float32)
        * query_scale
    )
    capped = softcap_value * jnp.tanh(scores / softcap_value)
    offsets = jnp.arange(rows, dtype=jnp.int32)
    query_pos = device_index * rows + offsets
    key_pos = source * rows + offsets
    distance = query_pos[:, None] - key_pos[None, :]
    allowed = (distance >= 0) & (distance < WINDOW_TOKENS) & (key_pos[None, :] >= 0)
    weights = jnp.where(allowed[None, None], jnp.exp(capped), 0.0)
    denominators = denominators + jnp.sum(weights, axis=-1)
    numerators = numerators + jnp.einsum(
        "grsk,kgh->grsh",
        weights.astype(jnp.bfloat16),
        value_block,
        preferred_element_type=jnp.float32,
    )
    return (numerators, denominators)


def along_lines(state, key_block, value_block, rotary_queries, device_index, cycle_size):
    kv_heads = key_block.shape[1]
    outer = cycle_size // 2
    forward = [(source, source + 2) for source in range(cycle_size - 2)]
    up = [(source, source + 1) for source in range(0, cycle_size, 2)]
    down = [(source + 1, source) for source in range(0, cycle_size, 2)]
    plane = device_index // 2
    side = device_index % 2

    def attend_stacked(state, stacked, source):
        return attend_block(
            state, stacked[:, :kv_heads], stacked[:, kv_heads:], source, rotary_queries, device_index
        )

    line = jnp.concatenate([key_block, value_block], axis=1)
    for step in range(1, outer + 1):
        if step < outer:
            arrived = lax.ppermute(line, "ctx", forward)
        crossed = lax.ppermute(line, "ctx", up if step == 1 else up + down)
        state = attend_stacked(state, crossed, 2 * (plane - step + 1) + 1 - side)
        if step < outer:
            state = attend_stacked(state, arrived, device_index - 2 * step)
            line = arrived
    return state


def exchanged(piece, count):
    pieces = [(piece, 0)]
    bit = count // 2
    while bit >= 1:
        sent = jnp.concatenate([held for held, unused in pieces], axis=1)
        arrived = lax.ppermute(sent, "tp", [(source, source ^ bit) for source in range(count)])
        width = piece.shape[1]
        pieces = pieces + [
            (arrived[:, slot * width : (slot + 1) * width], offset ^ bit)
            for slot, (unused, offset) in enumerate(pieces)
        ]
        bit //= 2
    return pieces


def summed(partial, count):
    bit = count // 2
    while bit >= 1:
        partial = partial + lax.ppermute(partial, "tp", [(source, source ^ bit) for source in range(count)])
        bit //= 2
    return partial


def local(queries, keys, values, residual, out_weight, post_gain):
    rows = queries.shape[0]
    q_heads = queries.shape[1]
    head_size = queries.shape[2]
    kv_heads = keys.shape[1]
    heads_per_group = q_heads // kv_heads
    cycle_size = lax.axis_size("ctx")
    device_index = lax.axis_index("ctx")
    positions = (device_index * rows + jnp.arange(rows, dtype=jnp.int32))[:, None]
    rotary_queries = rotate(queries.astype(jnp.float32), positions).astype(jnp.bfloat16)
    rotary_queries = rotary_queries.reshape(rows, kv_heads, heads_per_group, head_size)
    rotary_keys = rotate(keys.astype(jnp.float32), positions).astype(jnp.bfloat16)
    reach = min((WINDOW_TOKENS + rows - 2) // rows, cycle_size - 1)
    state = (
        jnp.zeros((kv_heads, heads_per_group, rows, head_size), jnp.float32),
        jnp.zeros((kv_heads, heads_per_group, rows), jnp.float32),
    )
    state = attend_block(state, rotary_keys, values, device_index, rotary_queries, device_index)
    if reach == cycle_size - 1 and cycle_size % 2 == 0:
        state = along_lines(state, rotary_keys, values, rotary_queries, device_index, cycle_size)
    elif reach > 0:

        def advance(step_index, carried):
            running, key_block, value_block = carried
            key_block, value_block = passed_along((key_block, value_block), "ctx", 1)
            running = attend_block(
                running,
                key_block,
                value_block,
                device_index - step_index - 1,
                rotary_queries,
                device_index,
            )
            return (running, key_block, value_block)

        state, unused_keys, unused_values = lax.fori_loop(
            0, reach, advance, (state, rotary_keys, values)
        )
    numerators, denominators = state
    attended = (numerators / denominators[..., None]).astype(jnp.bfloat16)
    attended = jnp.transpose(attended, (2, 0, 1, 3)).reshape(rows, q_heads, head_size)
    local_cols = out_weight.shape[2]
    tp_size = lax.axis_size("tp")
    tp_index = lax.axis_index("tp")
    butterfly = tp_size & (tp_size - 1) == 0
    if butterfly:
        projected = None
        for held, offset in exchanged(attended, tp_size):
            owner = jnp.bitwise_xor(tp_index, offset)
            weight_rows = lax.dynamic_slice_in_dim(out_weight, owner * q_heads, q_heads, 0)
            part = jnp.dot(
                held.reshape(rows, q_heads * head_size),
                weight_rows.reshape(q_heads * head_size, local_cols),
                preferred_element_type=jnp.float32,
            )
            projected = part if projected is None else projected + part
    else:
        piece = lax.all_gather(attended, "tp", axis=1, tiled=True)
        heads_in = piece.shape[1]
        weight_rows = out_weight.reshape(heads_in * head_size, local_cols)
        projected = jnp.dot(
            piece.reshape(rows, heads_in * head_size), weight_rows, preferred_element_type=jnp.float32
        )
    partial_sums = jnp.sum(projected * projected, axis=1)
    if butterfly:
        square_sums = summed(partial_sums, tp_size)
    else:
        square_sums = jnp.sum(lax.all_gather(partial_sums, "tp", axis=0), axis=0)
    normed = projected * lax.rsqrt(square_sums / D + 1e-06)[:, None] * post_gain.astype(jnp.float32)
    mixed = residual.astype(jnp.float32) + normed
    return mixed.astype(jnp.bfloat16)


def solution(mesh):
    in_specs = (
        P("ctx", "tp", None),
        P("ctx", "tp", None),
        P("ctx", "tp", None),
        P("ctx", "tp"),
        P(None, None, "tp"),
        P("tp"),
    )
    out_specs = P("ctx", "tp")
    return jax.shard_map(local, mesh=mesh, in_specs=in_specs, out_specs=out_specs, check_vma=False)
```

```python
import jax
import jax.numpy as jnp
from jax import lax
from jax.sharding import PartitionSpec as P

WINDOW_TOKENS = 4096
D = 3072


softcap_value = 50.0
query_scale = 1.0 / 12.0
rope_base = 10000.0


def passed_along(value, axis, steps):
    count = lax.axis_size(axis)
    first, last = (max(0, -steps), min(count, count - steps))
    return lax.ppermute(value, axis, [(source, source + steps) for source in range(first, last)])


def rotate(values_in, positions):
    half_width = values_in.shape[-1] // 2
    steps_half = jnp.arange(half_width, dtype=jnp.float32)
    inverse = rope_base ** (-2.0 * steps_half / values_in.shape[-1])
    angles = positions.astype(jnp.float32)[..., None] * inverse
    cosine = jnp.cos(angles)
    sine_part = jnp.sin(angles)
    first_half = values_in[..., :half_width]
    second_half = values_in[..., half_width:]
    return jnp.concatenate(
        [
            first_half * cosine - second_half * sine_part,
            second_half * cosine + first_half * sine_part,
        ],
        axis=-1,
    )


def attend_block(state, key_block, value_block, source, rotary_queries, device_index, whole=False):
    numerators, denominators = state
    rows = key_block.shape[0]
    scores = (
        jnp.einsum("sgrh,kgh->grsk", rotary_queries, key_block, preferred_element_type=jnp.float32)
        * query_scale
    )
    capped = softcap_value * jnp.tanh(scores / softcap_value)
    if whole:
        allowed = (source >= 0) & (source < device_index)
        weights = jnp.where(allowed, jnp.exp(capped), 0.0)
    else:
        offsets = jnp.arange(rows, dtype=jnp.int32)
        query_pos = device_index * rows + offsets
        key_pos = source * rows + offsets
        distance = query_pos[:, None] - key_pos[None, :]
        allowed = (distance >= 0) & (distance < WINDOW_TOKENS) & (key_pos[None, :] >= 0)
        weights = jnp.where(allowed[None, None], jnp.exp(capped), 0.0)
    denominators = denominators + jnp.sum(weights, axis=-1)
    numerators = numerators + jnp.einsum(
        "grsk,kgh->grsh",
        weights.astype(jnp.bfloat16),
        value_block,
        preferred_element_type=jnp.float32,
    )
    return (numerators, denominators)


def along_lines(state, key_block, value_block, rotary_queries, device_index, cycle_size):
    kv_heads = key_block.shape[1]
    outer = cycle_size // 2
    forward = [(source, source + 2) for source in range(cycle_size - 2)]
    up = [(source, source + 1) for source in range(0, cycle_size, 2)]
    down = [(source + 1, source) for source in range(0, cycle_size, 2)]
    plane = device_index // 2
    side = device_index % 2

    rows = key_block.shape[0]
    whole = cycle_size * rows - 1 < WINDOW_TOKENS

    def attend_stacked(state, stacked, source):
        return attend_block(
            state, stacked[:, :kv_heads], stacked[:, kv_heads:], source, rotary_queries, device_index, whole
        )

    line = jnp.concatenate([key_block, value_block], axis=1)
    for step in range(1, outer + 1):
        if step < outer:
            arrived = lax.ppermute(line, "ctx", forward)
        crossed = lax.ppermute(line, "ctx", up if step == 1 else up + down)
        state = attend_stacked(state, crossed, 2 * (plane - step + 1) + 1 - side)
        if step < outer:
            state = attend_stacked(state, arrived, device_index - 2 * step)
            line = arrived
    return state


def exchanged(piece, count):
    pieces = [(piece, 0)]
    bit = count // 2
    while bit >= 1:
        pairs = [(source, source ^ bit) for source in range(count)]
        pieces = pieces + [(lax.ppermute(held, "tp", pairs), offset ^ bit) for held, offset in pieces]
        bit //= 2
    return pieces


def summed(partial, count):
    bit = count // 2
    while bit >= 1:
        partial = partial + lax.ppermute(partial, "tp", [(source, source ^ bit) for source in range(count)])
        bit //= 2
    return partial


def local(queries, keys, values, residual, out_weight, post_gain):
    rows = queries.shape[0]
    q_heads = queries.shape[1]
    head_size = queries.shape[2]
    kv_heads = keys.shape[1]
    heads_per_group = q_heads // kv_heads
    cycle_size = lax.axis_size("ctx")
    device_index = lax.axis_index("ctx")
    positions = (device_index * rows + jnp.arange(rows, dtype=jnp.int32))[:, None]
    rotary_queries = rotate(queries.astype(jnp.float32), positions).astype(jnp.bfloat16)
    rotary_queries = rotary_queries.reshape(rows, kv_heads, heads_per_group, head_size)
    rotary_keys = rotate(keys.astype(jnp.float32), positions).astype(jnp.bfloat16)
    reach = min((WINDOW_TOKENS + rows - 2) // rows, cycle_size - 1)
    state = (
        jnp.zeros((kv_heads, heads_per_group, rows, head_size), jnp.float32),
        jnp.zeros((kv_heads, heads_per_group, rows), jnp.float32),
    )
    state = attend_block(state, rotary_keys, values, device_index, rotary_queries, device_index)
    if reach == cycle_size - 1 and cycle_size % 2 == 0:
        state = along_lines(state, rotary_keys, values, rotary_queries, device_index, cycle_size)
    elif reach > 0:

        def advance(step_index, carried):
            running, key_block, value_block = carried
            key_block, value_block = passed_along((key_block, value_block), "ctx", 1)
            running = attend_block(
                running,
                key_block,
                value_block,
                device_index - step_index - 1,
                rotary_queries,
                device_index,
            )
            return (running, key_block, value_block)

        state, unused_keys, unused_values = lax.fori_loop(
            0, reach, advance, (state, rotary_keys, values)
        )
    numerators, denominators = state
    attended = (numerators / denominators[..., None]).astype(jnp.bfloat16)
    attended = jnp.transpose(attended, (2, 0, 1, 3)).reshape(rows, q_heads, head_size)
    local_cols = out_weight.shape[2]
    tp_size = lax.axis_size("tp")
    tp_index = lax.axis_index("tp")
    butterfly = tp_size & (tp_size - 1) == 0
    if butterfly:
        projected = None
        for held, offset in exchanged(attended, tp_size):
            owner = jnp.bitwise_xor(tp_index, offset)
            weight_rows = lax.dynamic_slice_in_dim(out_weight, owner * q_heads, q_heads, 0)
            part = jnp.dot(
                held.reshape(rows, q_heads * head_size),
                weight_rows.reshape(q_heads * head_size, local_cols),
                preferred_element_type=jnp.float32,
            )
            projected = part if projected is None else projected + part
    else:
        piece = lax.all_gather(attended, "tp", axis=1, tiled=True)
        heads_in = piece.shape[1]
        weight_rows = out_weight.reshape(heads_in * head_size, local_cols)
        projected = jnp.dot(
            piece.reshape(rows, heads_in * head_size), weight_rows, preferred_element_type=jnp.float32
        )
    partial_sums = jnp.sum(projected * projected, axis=1)
    if butterfly:
        square_sums = summed(partial_sums, tp_size)
    else:
        square_sums = jnp.sum(lax.all_gather(partial_sums, "tp", axis=0), axis=0)
    normed = projected * lax.rsqrt(square_sums / D + 1e-06)[:, None] * post_gain.astype(jnp.float32)
    mixed = residual.astype(jnp.float32) + normed
    return mixed.astype(jnp.bfloat16)


def solution(mesh):
    in_specs = (
        P("ctx", "tp", None),
        P("ctx", "tp", None),
        P("ctx", "tp", None),
        P("ctx", "tp"),
        P(None, None, "tp"),
        P("tp"),
    )
    out_specs = P("ctx", "tp")
    return jax.shard_map(local, mesh=mesh, in_specs=in_specs, out_specs=out_specs, check_vma=False)
```

```python
import jax
import jax.numpy as jnp
from jax import lax
from jax.sharding import PartitionSpec as P

WINDOW_TOKENS = 4096
D = 3072


softcap_value = 50.0
query_scale = 1.0 / 12.0
rope_base = 10000.0


def passed_along(value, axis, steps):
    count = lax.axis_size(axis)
    first, last = (max(0, -steps), min(count, count - steps))
    return lax.ppermute(value, axis, [(source, source + steps) for source in range(first, last)])


def rotate(values_in, positions):
    half_width = values_in.shape[-1] // 2
    steps_half = jnp.arange(half_width, dtype=jnp.float32)
    inverse = rope_base ** (-2.0 * steps_half / values_in.shape[-1])
    angles = positions.astype(jnp.float32)[..., None] * inverse
    cosine = jnp.cos(angles)
    sine_part = jnp.sin(angles)
    first_half = values_in[..., :half_width]
    second_half = values_in[..., half_width:]
    return jnp.concatenate(
        [
            first_half * cosine - second_half * sine_part,
            second_half * cosine + first_half * sine_part,
        ],
        axis=-1,
    )


def attend_block(state, key_block, value_block, source, queries_by_group, device_index, whole=False):
    numerators, denominators = state
    rows = key_block.shape[0]
    if whole:
        allowed = (source >= 0) & (source < device_index)
    else:
        group_rows = queries_by_group[0].shape[0]
        query_pos = device_index * rows + jnp.arange(group_rows, dtype=jnp.int32) // (group_rows // rows)
        key_pos = source * rows + jnp.arange(rows, dtype=jnp.int32)
        distance = query_pos[:, None] - key_pos[None, :]
        allowed = (distance >= 0) & (distance < WINDOW_TOKENS) & (key_pos[None, :] >= 0)
    new_numerators = []
    new_denominators = []
    for group, group_queries in enumerate(queries_by_group):
        scores = (
            lax.dot_general(
                group_queries,
                key_block[:, group],
                (((1,), (1,)), ((), ())),
                preferred_element_type=jnp.float32,
            )
            * query_scale
        )
        capped = softcap_value * jnp.tanh(scores / softcap_value)
        weights = jnp.where(allowed, jnp.exp(capped), 0.0)
        new_denominators.append(denominators[group] + jnp.sum(weights, axis=-1))
        new_numerators.append(
            numerators[group]
            + jnp.dot(weights.astype(jnp.bfloat16), value_block[:, group], preferred_element_type=jnp.float32)
        )
    return (new_numerators, new_denominators)


def along_lines(state, key_block, value_block, rotary_queries, device_index, cycle_size):
    kv_heads = key_block.shape[1]
    outer = cycle_size // 2
    forward = [(source, source + 2) for source in range(cycle_size - 2)]
    up = [(source, source + 1) for source in range(0, cycle_size, 2)]
    down = [(source + 1, source) for source in range(0, cycle_size, 2)]
    plane = device_index // 2
    side = device_index % 2

    rows = key_block.shape[0]
    whole = cycle_size * rows - 1 < WINDOW_TOKENS

    def attend_stacked(state, stacked, source):
        return attend_block(
            state, stacked[:, :kv_heads], stacked[:, kv_heads:], source, rotary_queries, device_index, whole
        )

    line = jnp.concatenate([key_block, value_block], axis=1)
    for step in range(1, outer + 1):
        if step < outer:
            arrived = lax.ppermute(line, "ctx", forward)
        crossed = lax.ppermute(line, "ctx", up if step == 1 else up + down)
        state = attend_stacked(state, crossed, 2 * (plane - step + 1) + 1 - side)
        if step < outer:
            state = attend_stacked(state, arrived, device_index - 2 * step)
            line = arrived
    return state


def exchanged(piece, count):
    pieces = [(piece, 0)]
    bit = count // 2
    while bit >= 1:
        pairs = [(source, source ^ bit) for source in range(count)]
        pieces = pieces + [(lax.ppermute(held, "tp", pairs), offset ^ bit) for held, offset in pieces]
        bit //= 2
    return pieces


def summed(partial, count):
    total = partial
    for offset in range(1, count):
        total = total + lax.ppermute(partial, "tp", [(source, source ^ offset) for source in range(count)])
    return total


def local(queries, keys, values, residual, out_weight, post_gain):
    rows = queries.shape[0]
    q_heads = queries.shape[1]
    head_size = queries.shape[2]
    kv_heads = keys.shape[1]
    heads_per_group = q_heads // kv_heads
    cycle_size = lax.axis_size("ctx")
    device_index = lax.axis_index("ctx")
    positions = (device_index * rows + jnp.arange(rows, dtype=jnp.int32))[:, None]
    rotary_queries = rotate(queries.astype(jnp.float32), positions).astype(jnp.bfloat16)
    rotary_queries = rotary_queries.reshape(rows, kv_heads, heads_per_group, head_size)
    rotary_queries = [
        rotary_queries[:, group].reshape(rows * heads_per_group, head_size) for group in range(kv_heads)
    ]
    rotary_keys = rotate(keys.astype(jnp.float32), positions).astype(jnp.bfloat16)
    reach = min((WINDOW_TOKENS + rows - 2) // rows, cycle_size - 1)
    state = (
        [jnp.zeros((rows * heads_per_group, head_size), jnp.float32)] * kv_heads,
        [jnp.zeros((rows * heads_per_group,), jnp.float32)] * kv_heads,
    )
    state = attend_block(state, rotary_keys, values, device_index, rotary_queries, device_index)
    if reach == cycle_size - 1 and cycle_size % 2 == 0:
        state = along_lines(state, rotary_keys, values, rotary_queries, device_index, cycle_size)
    elif reach > 0:

        def advance(step_index, carried):
            running, key_block, value_block = carried
            key_block, value_block = passed_along((key_block, value_block), "ctx", 1)
            running = attend_block(
                running,
                key_block,
                value_block,
                device_index - step_index - 1,
                rotary_queries,
                device_index,
            )
            return (running, key_block, value_block)

        state, unused_keys, unused_values = lax.fori_loop(
            0, reach, advance, (state, rotary_keys, values)
        )
    numerators, denominators = state
    attended = jnp.stack(
        [
            (numerator / denominator[:, None]).astype(jnp.bfloat16).reshape(rows, heads_per_group, head_size)
            for numerator, denominator in zip(numerators, denominators)
        ],
        axis=1,
    ).reshape(rows, q_heads, head_size)
    local_cols = out_weight.shape[2]
    tp_size = lax.axis_size("tp")
    tp_index = lax.axis_index("tp")
    butterfly = tp_size & (tp_size - 1) == 0
    if butterfly:
        projected = None
        for held, offset in exchanged(attended, tp_size):
            owner = jnp.bitwise_xor(tp_index, offset)
            weight_rows = lax.dynamic_slice_in_dim(out_weight, owner * q_heads, q_heads, 0)
            part = jnp.dot(
                held.reshape(rows, q_heads * head_size),
                weight_rows.reshape(q_heads * head_size, local_cols),
                preferred_element_type=jnp.float32,
            )
            projected = part if projected is None else projected + part
    else:
        piece = lax.all_gather(attended, "tp", axis=1, tiled=True)
        heads_in = piece.shape[1]
        weight_rows = out_weight.reshape(heads_in * head_size, local_cols)
        projected = jnp.dot(
            piece.reshape(rows, heads_in * head_size), weight_rows, preferred_element_type=jnp.float32
        )
    partial_sums = jnp.sum(projected * projected, axis=1)
    if butterfly:
        square_sums = summed(partial_sums, tp_size)
    else:
        square_sums = jnp.sum(lax.all_gather(partial_sums, "tp", axis=0), axis=0)
    normed = projected * lax.rsqrt(square_sums / D + 1e-06)[:, None] * post_gain.astype(jnp.float32)
    mixed = residual.astype(jnp.float32) + normed
    return mixed.astype(jnp.bfloat16)


def solution(mesh):
    in_specs = (
        P("ctx", "tp", None),
        P("ctx", "tp", None),
        P("ctx", "tp", None),
        P("ctx", "tp"),
        P(None, None, "tp"),
        P("tp"),
    )
    out_specs = P("ctx", "tp")
    return jax.shard_map(local, mesh=mesh, in_specs=in_specs, out_specs=out_specs, check_vma=False)
```

```python
import jax
import jax.numpy as jnp
from jax import lax
from jax.sharding import PartitionSpec as P

WINDOW_TOKENS = 4096
D = 3072


softcap_value = 50.0
query_scale = 1.0 / 12.0
rope_base = 10000.0


def passed_along(value, axis, steps):
    count = lax.axis_size(axis)
    first, last = (max(0, -steps), min(count, count - steps))
    return lax.ppermute(value, axis, [(source, source + steps) for source in range(first, last)])


def rotate(values_in, positions):
    half_width = values_in.shape[-1] // 2
    steps_half = jnp.arange(half_width, dtype=jnp.float32)
    inverse = rope_base ** (-2.0 * steps_half / values_in.shape[-1])
    angles = positions.astype(jnp.float32)[..., None] * inverse
    cosine = jnp.cos(angles)
    sine_part = jnp.sin(angles)
    first_half = values_in[..., :half_width]
    second_half = values_in[..., half_width:]
    return jnp.concatenate(
        [
            first_half * cosine - second_half * sine_part,
            second_half * cosine + first_half * sine_part,
        ],
        axis=-1,
    )


def attend_block(state, key_block, value_block, source, rotary_queries, device_index, whole=False):
    numerators, denominators = state
    rows = key_block.shape[0]
    scores = (
        jnp.einsum("sgrh,kgh->grsk", rotary_queries, key_block, preferred_element_type=jnp.float32)
        * query_scale
    )
    capped = softcap_value * jnp.tanh(scores / softcap_value)
    if whole:
        allowed = (source >= 0) & (source < device_index)
        weights = jnp.where(allowed, jnp.exp(capped), 0.0)
    else:
        offsets = jnp.arange(rows, dtype=jnp.int32)
        query_pos = device_index * rows + offsets
        key_pos = source * rows + offsets
        distance = query_pos[:, None] - key_pos[None, :]
        allowed = (distance >= 0) & (distance < WINDOW_TOKENS) & (key_pos[None, :] >= 0)
        weights = jnp.where(allowed[None, None], jnp.exp(capped), 0.0)
    denominators = denominators + jnp.sum(weights, axis=-1)
    numerators = numerators + jnp.einsum(
        "grsk,kgh->grsh",
        weights.astype(jnp.bfloat16),
        value_block,
        preferred_element_type=jnp.float32,
    )
    return (numerators, denominators)


def along_lines(state, key_block, value_block, rotary_queries, device_index, cycle_size):
    kv_heads = key_block.shape[1]
    outer = cycle_size // 2
    def forward(step):
        return [(source, source + 2) for source in range(2 * step - 2, cycle_size - 2)]

    def across(step):
        pairs = [(2 * level, 2 * level + 1) for level in range(max(step - 1, 0), outer)]
        if step > 1:
            pairs = pairs + [(2 * level + 1, 2 * level) for level in range(step - 1, outer)]
        return pairs
    plane = device_index // 2
    side = device_index % 2

    rows = key_block.shape[0]
    whole = cycle_size * rows - 1 < WINDOW_TOKENS

    def attend_stacked(state, stacked, source):
        return attend_block(
            state, stacked[:, :kv_heads], stacked[:, kv_heads:], source, rotary_queries, device_index, whole
        )

    line = jnp.concatenate([key_block, value_block], axis=1)
    for step in range(1, outer + 1):
        if step < outer:
            arrived = lax.ppermute(line, "ctx", forward(step))
        crossed = lax.ppermute(line, "ctx", across(step))
        state = attend_stacked(state, crossed, 2 * (plane - step + 1) + 1 - side)
        if step < outer:
            state = attend_stacked(state, arrived, device_index - 2 * step)
            line = arrived
    return state


def exchanged(piece, count):
    pieces = [(piece, 0)]
    bit = count // 2
    while bit >= 1:
        pairs = [(source, source ^ bit) for source in range(count)]
        pieces = pieces + [(lax.ppermute(held, "tp", pairs), offset ^ bit) for held, offset in pieces]
        bit //= 2
    return pieces


def summed(partial, count):
    total = partial
    for offset in range(1, count):
        total = total + lax.ppermute(partial, "tp", [(source, source ^ offset) for source in range(count)])
    return total


def local(queries, keys, values, residual, out_weight, post_gain):
    rows = queries.shape[0]
    q_heads = queries.shape[1]
    head_size = queries.shape[2]
    kv_heads = keys.shape[1]
    heads_per_group = q_heads // kv_heads
    cycle_size = lax.axis_size("ctx")
    device_index = lax.axis_index("ctx")
    positions = (device_index * rows + jnp.arange(rows, dtype=jnp.int32))[:, None]
    rotary_queries = rotate(queries.astype(jnp.float32), positions).astype(jnp.bfloat16)
    rotary_queries = rotary_queries.reshape(rows, kv_heads, heads_per_group, head_size)
    rotary_keys = rotate(keys.astype(jnp.float32), positions).astype(jnp.bfloat16)
    reach = min((WINDOW_TOKENS + rows - 2) // rows, cycle_size - 1)
    state = (
        jnp.zeros((kv_heads, heads_per_group, rows, head_size), jnp.float32),
        jnp.zeros((kv_heads, heads_per_group, rows), jnp.float32),
    )
    state = attend_block(state, rotary_keys, values, device_index, rotary_queries, device_index)
    if reach == cycle_size - 1 and cycle_size % 2 == 0:
        state = along_lines(state, rotary_keys, values, rotary_queries, device_index, cycle_size)
    elif reach > 0:

        def advance(step_index, carried):
            running, key_block, value_block = carried
            key_block, value_block = passed_along((key_block, value_block), "ctx", 1)
            running = attend_block(
                running,
                key_block,
                value_block,
                device_index - step_index - 1,
                rotary_queries,
                device_index,
            )
            return (running, key_block, value_block)

        state, unused_keys, unused_values = lax.fori_loop(
            0, reach, advance, (state, rotary_keys, values)
        )
    numerators, denominators = state
    attended = (numerators / denominators[..., None]).astype(jnp.bfloat16)
    local_cols = out_weight.shape[2]
    tp_size = lax.axis_size("tp")
    tp_index = lax.axis_index("tp")
    butterfly = tp_size & (tp_size - 1) == 0
    if butterfly:
        projected = None
        for held, offset in exchanged(attended, tp_size):
            owner = jnp.bitwise_xor(tp_index, offset)
            weight_rows = lax.dynamic_slice_in_dim(out_weight, owner * q_heads, q_heads, 0)
            part = lax.dot_general(
                held,
                weight_rows.reshape(kv_heads, heads_per_group, head_size, local_cols),
                (((0, 1, 3), (0, 1, 2)), ((), ())),
                preferred_element_type=jnp.float32,
            )
            projected = part if projected is None else projected + part
    else:
        attended = jnp.transpose(attended, (2, 0, 1, 3)).reshape(rows, q_heads, head_size)
        piece = lax.all_gather(attended, "tp", axis=1, tiled=True)
        heads_in = piece.shape[1]
        weight_rows = out_weight.reshape(heads_in * head_size, local_cols)
        projected = jnp.dot(
            piece.reshape(rows, heads_in * head_size), weight_rows, preferred_element_type=jnp.float32
        )
    partial_sums = jnp.sum(projected * projected, axis=1)
    if butterfly:
        square_sums = summed(partial_sums, tp_size)
    else:
        square_sums = jnp.sum(lax.all_gather(partial_sums, "tp", axis=0), axis=0)
    normed = projected * lax.rsqrt(square_sums / D + 1e-06)[:, None] * post_gain.astype(jnp.float32)
    mixed = residual.astype(jnp.float32) + normed
    return mixed.astype(jnp.bfloat16)


def solution(mesh):
    in_specs = (
        P("ctx", "tp", None),
        P("ctx", "tp", None),
        P("ctx", "tp", None),
        P("ctx", "tp"),
        P(None, None, "tp"),
        P("tp"),
    )
    out_specs = P("ctx", "tp")
    return jax.shard_map(local, mesh=mesh, in_specs=in_specs, out_specs=out_specs, check_vma=False)
```

```python
import jax
import jax.numpy as jnp
from jax import lax
from jax.sharding import PartitionSpec as P

WINDOW_TOKENS = 4096
D = 3072


softcap_value = 50.0
query_scale = 1.0 / 12.0
rope_base = 10000.0


def passed_along(value, axis, steps):
    count = lax.axis_size(axis)
    first, last = (max(0, -steps), min(count, count - steps))
    return lax.ppermute(value, axis, [(source, source + steps) for source in range(first, last)])


def rotate(values_in, positions):
    half_width = values_in.shape[-1] // 2
    steps_half = jnp.arange(half_width, dtype=jnp.float32)
    inverse = rope_base ** (-2.0 * steps_half / values_in.shape[-1])
    angles = positions.astype(jnp.float32)[..., None] * inverse
    cosine = jnp.cos(angles)
    sine_part = jnp.sin(angles)
    first_half = values_in[..., :half_width]
    second_half = values_in[..., half_width:]
    return jnp.concatenate(
        [
            first_half * cosine - second_half * sine_part,
            second_half * cosine + first_half * sine_part,
        ],
        axis=-1,
    )


def attend_block(state, key_block, value_block, source, rotary_queries, device_index, whole=False):
    numerators, denominators = state
    rows = key_block.shape[0]
    scores = (
        jnp.einsum("sgrh,kgh->grsk", rotary_queries, key_block, preferred_element_type=jnp.float32)
        * query_scale
    )
    capped = softcap_value * jnp.tanh(scores / softcap_value)
    if whole:
        allowed = (source >= 0) & (source < device_index)
        weights = jnp.where(allowed, jnp.exp(capped), 0.0)
    else:
        offsets = jnp.arange(rows, dtype=jnp.int32)
        query_pos = device_index * rows + offsets
        key_pos = source * rows + offsets
        distance = query_pos[:, None] - key_pos[None, :]
        allowed = (distance >= 0) & (distance < WINDOW_TOKENS) & (key_pos[None, :] >= 0)
        weights = jnp.where(allowed[None, None], jnp.exp(capped), 0.0)
    denominators = denominators + jnp.sum(weights, axis=-1)
    numerators = numerators + jnp.einsum(
        "grsk,kgh->grsh",
        weights.astype(jnp.bfloat16),
        value_block,
        preferred_element_type=jnp.float32,
    )
    return (numerators, denominators)


def along_lines(state, key_block, value_block, rotary_queries, device_index, cycle_size):
    kv_heads = key_block.shape[1]
    outer = cycle_size // 2
    def forward(step):
        return [(source, source + 2) for source in range(2 * step - 2, cycle_size - 2)]

    def across(step):
        pairs = [(2 * level, 2 * level + 1) for level in range(max(step - 1, 0), outer)]
        if step > 1:
            pairs = pairs + [(2 * level + 1, 2 * level) for level in range(step - 1, outer)]
        return pairs
    plane = device_index // 2
    side = device_index % 2

    rows = key_block.shape[0]
    whole = cycle_size * rows - 1 < WINDOW_TOKENS

    def attend_stacked(state, stacked, source):
        return attend_block(
            state, stacked[:, :kv_heads], stacked[:, kv_heads:], source, rotary_queries, device_index, whole
        )

    line = jnp.concatenate([key_block, value_block], axis=1)
    for step in range(1, outer + 1):
        last_forward = step == outer - 1
        if step == outer and outer >= 2:
            break
        if step < outer:
            arrived = lax.ppermute(line, "ctx", forward(step))
        crossed = lax.ppermute(line, "ctx", across(step))
        if last_forward:
            diagonal = lax.ppermute(
                line,
                "ctx",
                [(source, 2 * (source // 2) + 3 - source % 2) for source, unused in forward(step)],
            )
        state = attend_stacked(state, crossed, 2 * (plane - step + 1) + 1 - side)
        if step < outer:
            state = attend_stacked(state, arrived, device_index - 2 * step)
            line = arrived
        if last_forward:
            state = attend_stacked(state, diagonal, 2 * (plane - step) + 1 - side)
    return state


def exchanged(piece, count):
    pieces = [(piece, 0)]
    bit = count // 2
    while bit >= 1:
        pairs = [(source, source ^ bit) for source in range(count)]
        pieces = pieces + [(lax.ppermute(held, "tp", pairs), offset ^ bit) for held, offset in pieces]
        bit //= 2
    return pieces


def summed(partial, count):
    total = partial
    for offset in range(1, count):
        total = total + lax.ppermute(partial, "tp", [(source, source ^ offset) for source in range(count)])
    return total


def local(queries, keys, values, residual, out_weight, post_gain):
    rows = queries.shape[0]
    q_heads = queries.shape[1]
    head_size = queries.shape[2]
    kv_heads = keys.shape[1]
    heads_per_group = q_heads // kv_heads
    cycle_size = lax.axis_size("ctx")
    device_index = lax.axis_index("ctx")
    positions = (device_index * rows + jnp.arange(rows, dtype=jnp.int32))[:, None]
    rotary_queries = rotate(queries.astype(jnp.float32), positions).astype(jnp.bfloat16)
    rotary_queries = rotary_queries.reshape(rows, kv_heads, heads_per_group, head_size)
    rotary_keys = rotate(keys.astype(jnp.float32), positions).astype(jnp.bfloat16)
    reach = min((WINDOW_TOKENS + rows - 2) // rows, cycle_size - 1)
    state = (
        jnp.zeros((kv_heads, heads_per_group, rows, head_size), jnp.float32),
        jnp.zeros((kv_heads, heads_per_group, rows), jnp.float32),
    )
    state = attend_block(state, rotary_keys, values, device_index, rotary_queries, device_index)
    if reach == cycle_size - 1 and cycle_size % 2 == 0:
        state = along_lines(state, rotary_keys, values, rotary_queries, device_index, cycle_size)
    elif reach > 0:

        def advance(step_index, carried):
            running, key_block, value_block = carried
            key_block, value_block = passed_along((key_block, value_block), "ctx", 1)
            running = attend_block(
                running,
                key_block,
                value_block,
                device_index - step_index - 1,
                rotary_queries,
                device_index,
            )
            return (running, key_block, value_block)

        state, unused_keys, unused_values = lax.fori_loop(
            0, reach, advance, (state, rotary_keys, values)
        )
    numerators, denominators = state
    attended = (numerators / denominators[..., None]).astype(jnp.bfloat16)
    local_cols = out_weight.shape[2]
    tp_size = lax.axis_size("tp")
    tp_index = lax.axis_index("tp")
    butterfly = tp_size & (tp_size - 1) == 0
    if butterfly:
        projected = None
        for held, offset in exchanged(attended, tp_size):
            owner = jnp.bitwise_xor(tp_index, offset)
            weight_rows = lax.dynamic_slice_in_dim(out_weight, owner * q_heads, q_heads, 0)
            part = lax.dot_general(
                held,
                weight_rows.reshape(kv_heads, heads_per_group, head_size, local_cols),
                (((0, 1, 3), (0, 1, 2)), ((), ())),
                preferred_element_type=jnp.float32,
            )
            projected = part if projected is None else projected + part
    else:
        attended = jnp.transpose(attended, (2, 0, 1, 3)).reshape(rows, q_heads, head_size)
        piece = lax.all_gather(attended, "tp", axis=1, tiled=True)
        heads_in = piece.shape[1]
        weight_rows = out_weight.reshape(heads_in * head_size, local_cols)
        projected = jnp.dot(
            piece.reshape(rows, heads_in * head_size), weight_rows, preferred_element_type=jnp.float32
        )
    partial_sums = jnp.sum(projected * projected, axis=1)
    if butterfly:
        square_sums = summed(partial_sums, tp_size)
    else:
        square_sums = jnp.sum(lax.all_gather(partial_sums, "tp", axis=0), axis=0)
    normed = projected * lax.rsqrt(square_sums / D + 1e-06)[:, None] * post_gain.astype(jnp.float32)
    mixed = residual.astype(jnp.float32) + normed
    return mixed.astype(jnp.bfloat16)


def solution(mesh):
    in_specs = (
        P("ctx", "tp", None),
        P("ctx", "tp", None),
        P("ctx", "tp", None),
        P("ctx", "tp"),
        P(None, None, "tp"),
        P("tp"),
    )
    out_specs = P("ctx", "tp")
    return jax.shard_map(local, mesh=mesh, in_specs=in_specs, out_specs=out_specs, check_vma=False)
```

```python
import jax
import jax.numpy as jnp
from jax import lax
from jax.sharding import PartitionSpec as P
from jax.experimental import pallas as pl

WINDOW_TOKENS = 4096
D = 3072


softcap_value = 50.0
query_scale = 1.0 / 12.0
rope_base = 10000.0


def passed_along(value, axis, steps):
    count = lax.axis_size(axis)
    first, last = (max(0, -steps), min(count, count - steps))
    return lax.ppermute(value, axis, [(source, source + steps) for source in range(first, last)])


def rotate(values_in, positions):
    half_width = values_in.shape[-1] // 2
    steps_half = jnp.arange(half_width, dtype=jnp.float32)
    inverse = rope_base ** (-2.0 * steps_half / values_in.shape[-1])
    angles = positions.astype(jnp.float32)[..., None] * inverse
    cosine = jnp.cos(angles)
    sine_part = jnp.sin(angles)
    first_half = values_in[..., :half_width]
    second_half = values_in[..., half_width:]
    return jnp.concatenate(
        [
            first_half * cosine - second_half * sine_part,
            second_half * cosine + first_half * sine_part,
        ],
        axis=-1,
    )


def attend_block(state, key_block, value_block, source, rotary_queries, device_index, whole=False):
    numerators, denominators = state
    rows = key_block.shape[0]
    scores = (
        jnp.einsum("sgrh,kgh->grsk", rotary_queries, key_block, preferred_element_type=jnp.float32)
        * query_scale
    )
    capped = softcap_value * jnp.tanh(scores / softcap_value)
    if whole:
        allowed = (source >= 0) & (source < device_index)
        weights = jnp.where(allowed, jnp.exp(capped), 0.0)
    else:
        offsets = jnp.arange(rows, dtype=jnp.int32)
        query_pos = device_index * rows + offsets
        key_pos = source * rows + offsets
        distance = query_pos[:, None] - key_pos[None, :]
        allowed = (distance >= 0) & (distance < WINDOW_TOKENS) & (key_pos[None, :] >= 0)
        weights = jnp.where(allowed[None, None], jnp.exp(capped), 0.0)
    denominators = denominators + jnp.sum(weights, axis=-1)
    numerators = numerators + jnp.einsum(
        "grsk,kgh->grsh",
        weights.astype(jnp.bfloat16),
        value_block,
        preferred_element_type=jnp.float32,
    )
    return (numerators, denominators)


def along_lines(state, line, rotary_queries, device_index, cycle_size):
    kv_heads = line.shape[1] // 2
    outer = cycle_size // 2
    def forward(step):
        return [(source, source + 2) for source in range(2 * step - 2, cycle_size - 2)]

    def across(step):
        pairs = [(2 * level, 2 * level + 1) for level in range(max(step - 1, 0), outer)]
        if step > 1:
            pairs = pairs + [(2 * level + 1, 2 * level) for level in range(step - 1, outer)]
        return pairs
    plane = device_index // 2
    side = device_index % 2

    rows = line.shape[0]
    whole = cycle_size * rows - 1 < WINDOW_TOKENS

    def attend_stacked(state, stacked, source):
        return attend_block(
            state, stacked[:, :kv_heads], stacked[:, kv_heads:], source, rotary_queries, device_index, whole
        )

    for step in range(1, outer + 1):
        last_forward = step == outer - 1
        if step == outer and outer >= 2:
            break
        if step < outer:
            arrived = lax.ppermute(line, "ctx", forward(step))
        crossed = lax.ppermute(line, "ctx", across(step))
        if last_forward:
            diagonal = lax.ppermute(
                line,
                "ctx",
                [(source, 2 * (source // 2) + 3 - source % 2) for source, unused in forward(step)],
            )
        state = attend_stacked(state, crossed, 2 * (plane - step + 1) + 1 - side)
        if step < outer:
            state = attend_stacked(state, arrived, device_index - 2 * step)
            line = arrived
        if last_forward:
            state = attend_stacked(state, diagonal, 2 * (plane - step) + 1 - side)
    return state


def exchanged(piece, count):
    pieces = [(piece, 0)]
    bit = count // 2
    while bit >= 1:
        pairs = [(source, source ^ bit) for source in range(count)]
        pieces = pieces + [(lax.ppermute(held, "tp", pairs), offset ^ bit) for held, offset in pieces]
        bit //= 2
    return pieces


def summed(partial, count):
    total = partial
    for offset in range(1, count):
        total = total + lax.ppermute(partial, "tp", [(source, source ^ offset) for source in range(count)])
    return total


def key_value_line(keys, values, positions):
    rows, kv_heads, head_size = keys.shape
    half_width = head_size // 2
    steps_half = jnp.arange(half_width, dtype=jnp.float32)
    inverse = rope_base ** (-2.0 * steps_half / head_size)
    angles = positions.astype(jnp.float32)[..., None] * inverse
    cosine = jnp.cos(angles)
    sine_part = jnp.sin(angles)

    def kernel(key_ref, value_ref, cosine_ref, sine_ref, out_ref):
        cos_block = cosine_ref[...]
        sin_block = sine_ref[...]
        for head in range(kv_heads):
            entries = key_ref[head].astype(jnp.float32)
            first_half = entries[:, :half_width]
            second_half = entries[:, half_width:]
            out_ref[head, :, :half_width] = (first_half * cos_block - second_half * sin_block).astype(out_ref.dtype)
            out_ref[head, :, half_width:] = (second_half * cos_block + first_half * sin_block).astype(out_ref.dtype)
            out_ref[kv_heads + head] = value_ref[head]

    head_major = pl.pallas_call(
        kernel,
        out_shape=jax.ShapeDtypeStruct((2 * kv_heads, rows, head_size), keys.dtype),
    )(jnp.transpose(keys, (1, 0, 2)), jnp.transpose(values, (1, 0, 2)), cosine, sine_part)
    return jnp.transpose(head_major, (1, 0, 2))


def local(queries, keys, values, residual, out_weight, post_gain):
    rows = queries.shape[0]
    q_heads = queries.shape[1]
    head_size = queries.shape[2]
    kv_heads = keys.shape[1]
    heads_per_group = q_heads // kv_heads
    cycle_size = lax.axis_size("ctx")
    device_index = lax.axis_index("ctx")
    positions = (device_index * rows + jnp.arange(rows, dtype=jnp.int32))[:, None]
    rotary_queries = rotate(queries.astype(jnp.float32), positions).astype(jnp.bfloat16)
    rotary_queries = rotary_queries.reshape(rows, kv_heads, heads_per_group, head_size)
    reach = min((WINDOW_TOKENS + rows - 2) // rows, cycle_size - 1)
    lines = reach == cycle_size - 1 and cycle_size % 2 == 0
    if lines:
        line = key_value_line(keys, values, positions[:, 0])
        rotary_keys = line[:, :kv_heads]
    else:
        rotary_keys = rotate(keys.astype(jnp.float32), positions).astype(jnp.bfloat16)
    state = (
        jnp.zeros((kv_heads, heads_per_group, rows, head_size), jnp.float32),
        jnp.zeros((kv_heads, heads_per_group, rows), jnp.float32),
    )
    state = attend_block(state, rotary_keys, values, device_index, rotary_queries, device_index)
    if lines:
        state = along_lines(state, line, rotary_queries, device_index, cycle_size)
    elif reach > 0:

        def advance(step_index, carried):
            running, key_block, value_block = carried
            key_block, value_block = passed_along((key_block, value_block), "ctx", 1)
            running = attend_block(
                running,
                key_block,
                value_block,
                device_index - step_index - 1,
                rotary_queries,
                device_index,
            )
            return (running, key_block, value_block)

        state, unused_keys, unused_values = lax.fori_loop(
            0, reach, advance, (state, rotary_keys, values)
        )
    numerators, denominators = state
    attended = (numerators / denominators[..., None]).astype(jnp.bfloat16)
    local_cols = out_weight.shape[2]
    tp_size = lax.axis_size("tp")
    tp_index = lax.axis_index("tp")
    butterfly = tp_size & (tp_size - 1) == 0
    if butterfly:
        projected = None
        for held, offset in exchanged(attended, tp_size):
            owner = jnp.bitwise_xor(tp_index, offset)
            weight_rows = lax.dynamic_slice_in_dim(out_weight, owner * q_heads, q_heads, 0)
            part = lax.dot_general(
                held,
                weight_rows.reshape(kv_heads, heads_per_group, head_size, local_cols),
                (((0, 1, 3), (0, 1, 2)), ((), ())),
                preferred_element_type=jnp.float32,
            )
            projected = part if projected is None else projected + part
    else:
        attended = jnp.transpose(attended, (2, 0, 1, 3)).reshape(rows, q_heads, head_size)
        piece = lax.all_gather(attended, "tp", axis=1, tiled=True)
        heads_in = piece.shape[1]
        weight_rows = out_weight.reshape(heads_in * head_size, local_cols)
        projected = jnp.dot(
            piece.reshape(rows, heads_in * head_size), weight_rows, preferred_element_type=jnp.float32
        )
    partial_sums = jnp.sum(projected * projected, axis=1)
    if butterfly:
        square_sums = summed(partial_sums, tp_size)
    else:
        square_sums = jnp.sum(lax.all_gather(partial_sums, "tp", axis=0), axis=0)
    normed = projected * lax.rsqrt(square_sums / D + 1e-06)[:, None] * post_gain.astype(jnp.float32)
    mixed = residual.astype(jnp.float32) + normed
    return mixed.astype(jnp.bfloat16)


def solution(mesh):
    in_specs = (
        P("ctx", "tp", None),
        P("ctx", "tp", None),
        P("ctx", "tp", None),
        P("ctx", "tp"),
        P(None, None, "tp"),
        P("tp"),
    )
    out_specs = P("ctx", "tp")
    return jax.shard_map(local, mesh=mesh, in_specs=in_specs, out_specs=out_specs, check_vma=False)
```

```python
import jax
import jax.numpy as jnp
from jax import lax
from jax.sharding import PartitionSpec as P

WINDOW_TOKENS = 4096
D = 3072


softcap_value = 50.0
query_scale = 1.0 / 12.0
rope_base = 10000.0


def passed_along(value, axis, steps):
    count = lax.axis_size(axis)
    first, last = (max(0, -steps), min(count, count - steps))
    return lax.ppermute(value, axis, [(source, source + steps) for source in range(first, last)])


def rotate(values_in, positions):
    half_width = values_in.shape[-1] // 2
    steps_half = jnp.arange(half_width, dtype=jnp.float32)
    inverse = rope_base ** (-2.0 * steps_half / values_in.shape[-1])
    angles = positions.astype(jnp.float32)[..., None] * inverse
    cosine = jnp.cos(angles)
    sine_part = jnp.sin(angles)
    first_half = values_in[..., :half_width]
    second_half = values_in[..., half_width:]
    return jnp.concatenate(
        [
            first_half * cosine - second_half * sine_part,
            second_half * cosine + first_half * sine_part,
        ],
        axis=-1,
    )


def attend_block(state, key_block, value_block, source, rotary_queries, device_index, whole=False):
    numerators, denominators = state
    rows = key_block.shape[0]
    scores = (
        jnp.einsum("sgrh,kgh->grsk", rotary_queries, key_block, preferred_element_type=jnp.float32)
        * query_scale
    )
    capped = softcap_value * jnp.tanh(scores / softcap_value)
    if whole:
        allowed = (source >= 0) & (source < device_index)
        weights = jnp.where(allowed, jnp.exp(capped), 0.0)
    else:
        offsets = jnp.arange(rows, dtype=jnp.int32)
        query_pos = device_index * rows + offsets
        key_pos = source * rows + offsets
        distance = query_pos[:, None] - key_pos[None, :]
        allowed = (distance >= 0) & (distance < WINDOW_TOKENS) & (key_pos[None, :] >= 0)
        weights = jnp.where(allowed[None, None], jnp.exp(capped), 0.0)
    denominators = denominators + jnp.sum(weights, axis=-1)
    numerators = numerators + jnp.einsum(
        "grsk,kgh->grsh",
        weights.astype(jnp.bfloat16),
        value_block,
        preferred_element_type=jnp.float32,
    )
    return (numerators, denominators)


def along_lines(state, key_block, value_block, rotary_queries, device_index, cycle_size):
    kv_heads = key_block.shape[1]
    outer = cycle_size // 2
    def forward(step):
        return [(source, source + 2) for source in range(2 * step - 2, cycle_size - 2)]

    def across(step):
        pairs = [(2 * level, 2 * level + 1) for level in range(max(step - 1, 0), outer)]
        if step > 1:
            pairs = pairs + [(2 * level + 1, 2 * level) for level in range(step - 1, outer)]
        return pairs
    plane = device_index // 2
    side = device_index % 2

    rows = key_block.shape[0]
    whole = cycle_size * rows - 1 < WINDOW_TOKENS

    def attend_stacked(state, stacked, source):
        return attend_block(
            state, stacked[:, :kv_heads], stacked[:, kv_heads:], source, rotary_queries, device_index, whole
        )

    line = jnp.concatenate([key_block, value_block], axis=1)
    for step in range(1, outer + 1):
        last_forward = step == outer - 1
        if step == outer and outer >= 2:
            break
        if step < outer:
            arrived = lax.ppermute(line, "ctx", forward(step))
        crossed = lax.ppermute(line, "ctx", across(step))
        if last_forward:
            diagonal = lax.ppermute(
                line,
                "ctx",
                [(source, 2 * (source // 2) + 3 - source % 2) for source, unused in forward(step)],
            )
        state = attend_stacked(state, crossed, 2 * (plane - step + 1) + 1 - side)
        if step < outer:
            state = attend_stacked(state, arrived, device_index - 2 * step)
            line = arrived
        if last_forward:
            state = attend_stacked(state, diagonal, 2 * (plane - step) + 1 - side)
    return state


def exchanged(piece, count):
    pieces = [(piece, 0)]
    bit = count // 2
    while bit >= 1:
        pairs = [(source, source ^ bit) for source in range(count)]
        pieces = pieces + [(lax.ppermute(held, "tp", pairs), offset ^ bit) for held, offset in pieces]
        bit //= 2
    return pieces


def summed(partial, count):
    total = partial
    for offset in range(1, count):
        total = total + lax.ppermute(partial, "tp", [(source, source ^ offset) for source in range(count)])
    return total


def with_helpers(state, line, rotary_queries, device_index, cycle_size):
    kv_heads = line.shape[1] // 2
    rows = line.shape[0]
    whole = cycle_size * rows - 1 < WINDOW_TOKENS
    plane = device_index // 2
    side = device_index % 2
    back = cycle_size // 2

    def attend_stacked(state, stacked, source, queries, owner):
        return attend_block(
            state, stacked[:, :kv_heads], stacked[:, kv_heads:], source, queries, owner, whole
        )

    foreign = lax.ppermute(rotary_queries, "ctx", [(source, source - back) for source in range(back, cycle_size)])
    ahead = lax.ppermute(line, "ctx", [(source, source + 2) for source in range(cycle_size - 2)])
    slanted = lax.ppermute(
        line, "ctx", [(source, 2 * (source // 2) + 3 - source % 2) for source in range(cycle_size - 2)]
    )
    across = [(2 * level, 2 * level + 1) for level in range(back)]
    across = across + [(2 * level + 1, 2 * level) for level in range(back // 2)]
    crossed = lax.ppermute(line, "ctx", across)
    sources = (
        (crossed, 2 * plane + 1 - side),
        (ahead, device_index - 2),
        (slanted, 2 * (plane - 1) + 1 - side),
    )
    for stacked, source in sources:
        state = attend_stacked(state, stacked, source, rotary_queries, device_index)

    numerators, denominators = state
    owner = device_index + back

    def help_later():
        partial = (jnp.zeros_like(numerators), jnp.zeros_like(denominators))
        partial = attend_stacked(partial, line, device_index, foreign, owner)
        for stacked, source in sources:
            partial = attend_stacked(partial, stacked, source, foreign, owner)
        return partial

    def no_help():
        return (jnp.zeros_like(numerators), jnp.zeros_like(denominators))

    partial_numerators, partial_denominators = lax.cond(device_index < back, help_later, no_help)
    returned = [(source, source + back) for source in range(back)]
    far_numerators = lax.ppermute(partial_numerators.astype(jnp.bfloat16), "ctx", returned)
    far_denominators = lax.ppermute(partial_denominators, "ctx", returned)
    return (numerators + far_numerators.astype(jnp.float32), denominators + far_denominators)


def local(queries, keys, values, residual, out_weight, post_gain):
    rows = queries.shape[0]
    q_heads = queries.shape[1]
    head_size = queries.shape[2]
    kv_heads = keys.shape[1]
    heads_per_group = q_heads // kv_heads
    cycle_size = lax.axis_size("ctx")
    device_index = lax.axis_index("ctx")
    positions = (device_index * rows + jnp.arange(rows, dtype=jnp.int32))[:, None]
    rotary_queries = rotate(queries.astype(jnp.float32), positions).astype(jnp.bfloat16)
    rotary_queries = rotary_queries.reshape(rows, kv_heads, heads_per_group, head_size)
    rotary_keys = rotate(keys.astype(jnp.float32), positions).astype(jnp.bfloat16)
    reach = min((WINDOW_TOKENS + rows - 2) // rows, cycle_size - 1)
    state = (
        jnp.zeros((kv_heads, heads_per_group, rows, head_size), jnp.float32),
        jnp.zeros((kv_heads, heads_per_group, rows), jnp.float32),
    )
    state = attend_block(state, rotary_keys, values, device_index, rotary_queries, device_index)
    if reach == cycle_size - 1 and cycle_size == 8 and cycle_size * rows - 1 < WINDOW_TOKENS:
        line = jnp.concatenate([rotary_keys, values], axis=1)
        state = with_helpers(state, line, rotary_queries, device_index, cycle_size)
    elif reach == cycle_size - 1 and cycle_size % 2 == 0:
        state = along_lines(state, rotary_keys, values, rotary_queries, device_index, cycle_size)
    elif reach > 0:

        def advance(step_index, carried):
            running, key_block, value_block = carried
            key_block, value_block = passed_along((key_block, value_block), "ctx", 1)
            running = attend_block(
                running,
                key_block,
                value_block,
                device_index - step_index - 1,
                rotary_queries,
                device_index,
            )
            return (running, key_block, value_block)

        state, unused_keys, unused_values = lax.fori_loop(
            0, reach, advance, (state, rotary_keys, values)
        )
    numerators, denominators = state
    attended = (numerators / denominators[..., None]).astype(jnp.bfloat16)
    local_cols = out_weight.shape[2]
    tp_size = lax.axis_size("tp")
    tp_index = lax.axis_index("tp")
    butterfly = tp_size & (tp_size - 1) == 0
    if butterfly:
        projected = None
        for held, offset in exchanged(attended, tp_size):
            owner = jnp.bitwise_xor(tp_index, offset)
            weight_rows = lax.dynamic_slice_in_dim(out_weight, owner * q_heads, q_heads, 0)
            part = lax.dot_general(
                held,
                weight_rows.reshape(kv_heads, heads_per_group, head_size, local_cols),
                (((0, 1, 3), (0, 1, 2)), ((), ())),
                preferred_element_type=jnp.float32,
            )
            projected = part if projected is None else projected + part
    else:
        attended = jnp.transpose(attended, (2, 0, 1, 3)).reshape(rows, q_heads, head_size)
        piece = lax.all_gather(attended, "tp", axis=1, tiled=True)
        heads_in = piece.shape[1]
        weight_rows = out_weight.reshape(heads_in * head_size, local_cols)
        projected = jnp.dot(
            piece.reshape(rows, heads_in * head_size), weight_rows, preferred_element_type=jnp.float32
        )
    partial_sums = jnp.sum(projected * projected, axis=1)
    if butterfly:
        square_sums = summed(partial_sums, tp_size)
    else:
        square_sums = jnp.sum(lax.all_gather(partial_sums, "tp", axis=0), axis=0)
    normed = projected * lax.rsqrt(square_sums / D + 1e-06)[:, None] * post_gain.astype(jnp.float32)
    mixed = residual.astype(jnp.float32) + normed
    return mixed.astype(jnp.bfloat16)


def solution(mesh):
    in_specs = (
        P("ctx", "tp", None),
        P("ctx", "tp", None),
        P("ctx", "tp", None),
        P("ctx", "tp"),
        P(None, None, "tp"),
        P("tp"),
    )
    out_specs = P("ctx", "tp")
    return jax.shard_map(local, mesh=mesh, in_specs=in_specs, out_specs=out_specs, check_vma=False)
```

```python
import jax
import jax.numpy as jnp
from jax import lax
from jax.sharding import PartitionSpec as P

WINDOW_TOKENS = 4096
D = 3072


softcap_value = 50.0
query_scale = 1.0 / 12.0
rope_base = 10000.0


def passed_along(value, axis, steps):
    count = lax.axis_size(axis)
    first, last = (max(0, -steps), min(count, count - steps))
    return lax.ppermute(value, axis, [(source, source + steps) for source in range(first, last)])


def rotate(values_in, positions):
    half_width = values_in.shape[-1] // 2
    steps_half = jnp.arange(half_width, dtype=jnp.float32)
    inverse = rope_base ** (-2.0 * steps_half / values_in.shape[-1])
    angles = positions.astype(jnp.float32)[..., None] * inverse
    cosine = jnp.cos(angles)
    sine_part = jnp.sin(angles)
    first_half = values_in[..., :half_width]
    second_half = values_in[..., half_width:]
    return jnp.concatenate(
        [
            first_half * cosine - second_half * sine_part,
            second_half * cosine + first_half * sine_part,
        ],
        axis=-1,
    )


def attend_block(state, key_block, value_block, source, rotary_queries, device_index, whole=False):
    numerators, denominators = state
    rows = key_block.shape[0]
    scores = (
        jnp.einsum("sgrh,kgh->grsk", rotary_queries, key_block, preferred_element_type=jnp.float32)
        * query_scale
    )
    capped = softcap_value * jnp.tanh(scores / softcap_value)
    if whole:
        allowed = (source >= 0) & (source < device_index)
        weights = jnp.where(allowed, jnp.exp(capped), 0.0)
    else:
        offsets = jnp.arange(rows, dtype=jnp.int32)
        query_pos = device_index * rows + offsets
        key_pos = source * rows + offsets
        distance = query_pos[:, None] - key_pos[None, :]
        allowed = (distance >= 0) & (distance < WINDOW_TOKENS) & (key_pos[None, :] >= 0)
        weights = jnp.where(allowed[None, None], jnp.exp(capped), 0.0)
    denominators = denominators + jnp.sum(weights, axis=-1)
    numerators = numerators + jnp.einsum(
        "grsk,kgh->grsh",
        weights.astype(jnp.bfloat16),
        value_block,
        preferred_element_type=jnp.float32,
    )
    return (numerators, denominators)


def along_lines(state, key_block, value_block, rotary_queries, device_index, cycle_size):
    kv_heads = key_block.shape[1]
    outer = cycle_size // 2
    def forward(step):
        return [(source, source + 2) for source in range(2 * step - 2, cycle_size - 2)]

    def across(step):
        pairs = [(2 * level, 2 * level + 1) for level in range(max(step - 1, 0), outer)]
        if step > 1:
            pairs = pairs + [(2 * level + 1, 2 * level) for level in range(step - 1, outer)]
        return pairs
    plane = device_index // 2
    side = device_index % 2

    rows = key_block.shape[0]
    whole = cycle_size * rows - 1 < WINDOW_TOKENS

    offsets = jnp.arange(rows, dtype=jnp.int32)

    def attend_stacked(state, stacked, source):
        positions = (source * rows + offsets)[:, None]
        rotary_block = rotate(stacked[:, :kv_heads].astype(jnp.float32), positions).astype(jnp.bfloat16)
        return attend_block(
            state, rotary_block, stacked[:, kv_heads:], source, rotary_queries, device_index, whole
        )

    line = jnp.concatenate([key_block, value_block], axis=1)
    for step in range(1, outer + 1):
        last_forward = step == outer - 1
        if step == outer and outer >= 2:
            break
        if step < outer:
            arrived = lax.ppermute(line, "ctx", forward(step))
        crossed = lax.ppermute(line, "ctx", across(step))
        if last_forward:
            diagonal = lax.ppermute(
                line,
                "ctx",
                [(source, 2 * (source // 2) + 3 - source % 2) for source, unused in forward(step)],
            )
        state = attend_stacked(state, crossed, 2 * (plane - step + 1) + 1 - side)
        if step < outer:
            state = attend_stacked(state, arrived, device_index - 2 * step)
            line = arrived
        if last_forward:
            state = attend_stacked(state, diagonal, 2 * (plane - step) + 1 - side)
    return state


def exchanged(piece, count):
    pieces = [(piece, 0)]
    bit = count // 2
    while bit >= 1:
        pairs = [(source, source ^ bit) for source in range(count)]
        pieces = pieces + [(lax.ppermute(held, "tp", pairs), offset ^ bit) for held, offset in pieces]
        bit //= 2
    return pieces


def summed(partial, count):
    total = partial
    for offset in range(1, count):
        total = total + lax.ppermute(partial, "tp", [(source, source ^ offset) for source in range(count)])
    return total


def local(queries, keys, values, residual, out_weight, post_gain):
    rows = queries.shape[0]
    q_heads = queries.shape[1]
    head_size = queries.shape[2]
    kv_heads = keys.shape[1]
    heads_per_group = q_heads // kv_heads
    cycle_size = lax.axis_size("ctx")
    device_index = lax.axis_index("ctx")
    positions = (device_index * rows + jnp.arange(rows, dtype=jnp.int32))[:, None]
    rotary_queries = rotate(queries.astype(jnp.float32), positions).astype(jnp.bfloat16)
    rotary_queries = rotary_queries.reshape(rows, kv_heads, heads_per_group, head_size)
    rotary_keys = rotate(keys.astype(jnp.float32), positions).astype(jnp.bfloat16)
    reach = min((WINDOW_TOKENS + rows - 2) // rows, cycle_size - 1)
    state = (
        jnp.zeros((kv_heads, heads_per_group, rows, head_size), jnp.float32),
        jnp.zeros((kv_heads, heads_per_group, rows), jnp.float32),
    )
    state = attend_block(state, rotary_keys, values, device_index, rotary_queries, device_index)
    if reach == cycle_size - 1 and cycle_size % 2 == 0:
        state = along_lines(state, keys, values, rotary_queries, device_index, cycle_size)
    elif reach > 0:

        def advance(step_index, carried):
            running, key_block, value_block = carried
            key_block, value_block = passed_along((key_block, value_block), "ctx", 1)
            running = attend_block(
                running,
                key_block,
                value_block,
                device_index - step_index - 1,
                rotary_queries,
                device_index,
            )
            return (running, key_block, value_block)

        state, unused_keys, unused_values = lax.fori_loop(
            0, reach, advance, (state, rotary_keys, values)
        )
    numerators, denominators = state
    attended = (numerators / denominators[..., None]).astype(jnp.bfloat16)
    local_cols = out_weight.shape[2]
    tp_size = lax.axis_size("tp")
    tp_index = lax.axis_index("tp")
    butterfly = tp_size & (tp_size - 1) == 0
    if butterfly:
        projected = None
        for held, offset in exchanged(attended, tp_size):
            owner = jnp.bitwise_xor(tp_index, offset)
            weight_rows = lax.dynamic_slice_in_dim(out_weight, owner * q_heads, q_heads, 0)
            part = lax.dot_general(
                held,
                weight_rows.reshape(kv_heads, heads_per_group, head_size, local_cols),
                (((0, 1, 3), (0, 1, 2)), ((), ())),
                preferred_element_type=jnp.float32,
            )
            projected = part if projected is None else projected + part
    else:
        attended = jnp.transpose(attended, (2, 0, 1, 3)).reshape(rows, q_heads, head_size)
        piece = lax.all_gather(attended, "tp", axis=1, tiled=True)
        heads_in = piece.shape[1]
        weight_rows = out_weight.reshape(heads_in * head_size, local_cols)
        projected = jnp.dot(
            piece.reshape(rows, heads_in * head_size), weight_rows, preferred_element_type=jnp.float32
        )
    partial_sums = jnp.sum(projected * projected, axis=1)
    if butterfly:
        square_sums = summed(partial_sums, tp_size)
    else:
        square_sums = jnp.sum(lax.all_gather(partial_sums, "tp", axis=0), axis=0)
    normed = projected * lax.rsqrt(square_sums / D + 1e-06)[:, None] * post_gain.astype(jnp.float32)
    mixed = residual.astype(jnp.float32) + normed
    return mixed.astype(jnp.bfloat16)


def solution(mesh):
    in_specs = (
        P("ctx", "tp", None),
        P("ctx", "tp", None),
        P("ctx", "tp", None),
        P("ctx", "tp"),
        P(None, None, "tp"),
        P("tp"),
    )
    out_specs = P("ctx", "tp")
    return jax.shard_map(local, mesh=mesh, in_specs=in_specs, out_specs=out_specs, check_vma=False)
```

```python
import jax
import jax.numpy as jnp
from jax import lax
from jax.sharding import PartitionSpec as P

WINDOW_TOKENS = 4096
D = 3072


softcap_value = 50.0
query_scale = 1.0 / 12.0
rope_base = 10000.0


def passed_along(value, axis, steps):
    count = lax.axis_size(axis)
    first, last = (max(0, -steps), min(count, count - steps))
    return lax.ppermute(value, axis, [(source, source + steps) for source in range(first, last)])


def rotate(values_in, positions):
    half_width = values_in.shape[-1] // 2
    steps_half = jnp.arange(half_width, dtype=jnp.float32)
    inverse = rope_base ** (-2.0 * steps_half / values_in.shape[-1])
    angles = positions.astype(jnp.float32)[..., None] * inverse
    cosine = jnp.cos(angles)
    sine_part = jnp.sin(angles)
    first_half = values_in[..., :half_width]
    second_half = values_in[..., half_width:]
    return jnp.concatenate(
        [
            first_half * cosine - second_half * sine_part,
            second_half * cosine + first_half * sine_part,
        ],
        axis=-1,
    )


def attend_block(state, key_block, value_block, source, rotary_queries, device_index, whole=False):
    numerators, denominators = state
    rows = key_block.shape[0]
    scores = (
        jnp.einsum("sgrh,kgh->grsk", rotary_queries, key_block, preferred_element_type=jnp.float32)
        * query_scale
    )
    capped = softcap_value * jnp.tanh(scores / softcap_value)
    if whole:
        allowed = (source >= 0) & (source < device_index)
        weights = jnp.where(allowed, jnp.exp(capped), 0.0)
    else:
        offsets = jnp.arange(rows, dtype=jnp.int32)
        query_pos = device_index * rows + offsets
        key_pos = source * rows + offsets
        distance = query_pos[:, None] - key_pos[None, :]
        allowed = (distance >= 0) & (distance < WINDOW_TOKENS) & (key_pos[None, :] >= 0)
        weights = jnp.where(allowed[None, None], jnp.exp(capped), 0.0)
    denominators = denominators + jnp.sum(weights, axis=-1)
    numerators = numerators + jnp.einsum(
        "grsk,kgh->grsh",
        weights.astype(jnp.bfloat16),
        value_block,
        preferred_element_type=jnp.float32,
    )
    return (numerators, denominators)


def along_lines(state, key_block, value_block, rotary_queries, device_index, cycle_size):
    kv_heads = key_block.shape[1]
    outer = cycle_size // 2
    def forward(step):
        return [(source, source + 2) for source in range(2 * step - 2, cycle_size - 2)]

    def across(step):
        pairs = [(2 * level, 2 * level + 1) for level in range(max(step - 1, 0), outer)]
        if step > 1:
            pairs = pairs + [(2 * level + 1, 2 * level) for level in range(step - 1, outer)]
        return pairs
    plane = device_index // 2
    side = device_index % 2

    rows = key_block.shape[0]
    whole = cycle_size * rows - 1 < WINDOW_TOKENS

    def attend_stacked(state, stacked, source):
        return attend_block(
            state, stacked[:, :kv_heads], stacked[:, kv_heads:], source, rotary_queries, device_index, whole
        )

    line = jnp.concatenate([key_block, value_block], axis=1)
    for step in range(1, outer + 1):
        last_forward = step == outer - 1
        if step == outer and outer >= 2:
            break
        if step < outer:
            arrived = lax.ppermute(line, "ctx", forward(step))
        crossed = lax.ppermute(line, "ctx", across(step))
        if last_forward:
            diagonal = lax.ppermute(
                line,
                "ctx",
                [(source, 2 * (source // 2) + 3 - source % 2) for source, unused in forward(step)],
            )
        state = attend_stacked(state, crossed, 2 * (plane - step + 1) + 1 - side)
        if step < outer:
            state = attend_stacked(state, arrived, device_index - 2 * step)
            line = arrived
        if last_forward:
            state = attend_stacked(state, diagonal, 2 * (plane - step) + 1 - side)
    return state


def exchanged(piece, count):
    pieces = [(piece, 0)]
    bit = count // 2
    while bit >= 1:
        pairs = [(source, source ^ bit) for source in range(count)]
        pieces = pieces + [(lax.ppermute(held, "tp", pairs), offset ^ bit) for held, offset in pieces]
        bit //= 2
    return pieces


def summed(partial, count):
    total = partial
    for offset in range(1, count):
        total = total + lax.ppermute(partial, "tp", [(source, source ^ offset) for source in range(count)])
    return total


def local(queries, keys, values, residual, out_weight, post_gain):
    rows = queries.shape[0]
    q_heads = queries.shape[1]
    head_size = queries.shape[2]
    kv_heads = keys.shape[1]
    heads_per_group = q_heads // kv_heads
    cycle_size = lax.axis_size("ctx")
    device_index = lax.axis_index("ctx")
    positions = (device_index * rows + jnp.arange(rows, dtype=jnp.int32))[:, None]
    rotary_queries = rotate(queries.astype(jnp.float32), positions).astype(jnp.bfloat16)
    rotary_queries = rotary_queries.reshape(rows, kv_heads, heads_per_group, head_size)
    rotary_keys = rotate(keys.astype(jnp.float32), positions).astype(jnp.bfloat16)
    reach = min((WINDOW_TOKENS + rows - 2) // rows, cycle_size - 1)
    state = (
        jnp.zeros((kv_heads, heads_per_group, rows, head_size), jnp.float32),
        jnp.zeros((kv_heads, heads_per_group, rows), jnp.float32),
    )
    state = attend_block(state, rotary_keys, values, device_index, rotary_queries, device_index)
    if reach == cycle_size - 1 and cycle_size % 2 == 0:
        state = along_lines(state, rotary_keys, values, rotary_queries, device_index, cycle_size)
    elif reach > 0:

        def advance(step_index, carried):
            running, key_block, value_block = carried
            key_block, value_block = passed_along((key_block, value_block), "ctx", 1)
            running = attend_block(
                running,
                key_block,
                value_block,
                device_index - step_index - 1,
                rotary_queries,
                device_index,
            )
            return (running, key_block, value_block)

        state, unused_keys, unused_values = lax.fori_loop(
            0, reach, advance, (state, rotary_keys, values)
        )
    numerators, denominators = state
    attended = (numerators / denominators[..., None]).astype(jnp.bfloat16)
    local_cols = out_weight.shape[2]
    tp_size = lax.axis_size("tp")
    tp_index = lax.axis_index("tp")
    butterfly = tp_size & (tp_size - 1) == 0
    gain = post_gain.astype(jnp.float32)
    if butterfly and rows % 16 == 0:
        halves = []
        half_rows = rows // 2
        for part_index in range(2):
            block = attended[:, :, part_index * half_rows : (part_index + 1) * half_rows]
            projected = None
            for held, offset in exchanged(block, tp_size):
                owner = jnp.bitwise_xor(tp_index, offset)
                weight_rows = lax.dynamic_slice_in_dim(out_weight, owner * q_heads, q_heads, 0)
                part = lax.dot_general(
                    held,
                    weight_rows.reshape(kv_heads, heads_per_group, head_size, local_cols),
                    (((0, 1, 3), (0, 1, 2)), ((), ())),
                    preferred_element_type=jnp.float32,
                )
                projected = part if projected is None else projected + part
            square_sums = summed(jnp.sum(projected * projected, axis=1), tp_size)
            normed = projected * lax.rsqrt(square_sums / D + 1e-06)[:, None] * gain
            rows_in = residual[part_index * half_rows : (part_index + 1) * half_rows]
            halves.append((rows_in.astype(jnp.float32) + normed).astype(jnp.bfloat16))
        return jnp.concatenate(halves, axis=0)
    attended = jnp.transpose(attended, (2, 0, 1, 3)).reshape(rows, q_heads, head_size)
    piece = lax.all_gather(attended, "tp", axis=1, tiled=True)
    heads_in = piece.shape[1]
    weight_rows = out_weight.reshape(heads_in * head_size, local_cols)
    projected = jnp.dot(
        piece.reshape(rows, heads_in * head_size), weight_rows, preferred_element_type=jnp.float32
    )
    partial_sums = jnp.sum(projected * projected, axis=1)
    square_sums = jnp.sum(lax.all_gather(partial_sums, "tp", axis=0), axis=0)
    normed = projected * lax.rsqrt(square_sums / D + 1e-06)[:, None] * gain
    mixed = residual.astype(jnp.float32) + normed
    return mixed.astype(jnp.bfloat16)


def solution(mesh):
    in_specs = (
        P("ctx", "tp", None),
        P("ctx", "tp", None),
        P("ctx", "tp", None),
        P("ctx", "tp"),
        P(None, None, "tp"),
        P("tp"),
    )
    out_specs = P("ctx", "tp")
    return jax.shard_map(local, mesh=mesh, in_specs=in_specs, out_specs=out_specs, check_vma=False)
```

```python
import jax
import jax.numpy as jnp
from jax import lax
from jax.sharding import PartitionSpec as P

WINDOW_TOKENS = 4096
D = 3072


softcap_value = 50.0
query_scale = 1.0 / 12.0
rope_base = 10000.0


def passed_along(value, axis, steps):
    count = lax.axis_size(axis)
    first, last = (max(0, -steps), min(count, count - steps))
    return lax.ppermute(value, axis, [(source, source + steps) for source in range(first, last)])


def rotate(values_in, positions):
    half_width = values_in.shape[-1] // 2
    steps_half = jnp.arange(half_width, dtype=jnp.float32)
    inverse = rope_base ** (-2.0 * steps_half / values_in.shape[-1])
    angles = positions.astype(jnp.float32)[..., None] * inverse
    cosine = jnp.cos(angles)
    sine_part = jnp.sin(angles)
    first_half = values_in[..., :half_width]
    second_half = values_in[..., half_width:]
    return jnp.concatenate(
        [
            first_half * cosine - second_half * sine_part,
            second_half * cosine + first_half * sine_part,
        ],
        axis=-1,
    )


def attend_block(state, key_block, value_block, source, rotary_queries, device_index, whole=False):
    numerators, denominators = state
    rows = key_block.shape[0]
    scores = (
        jnp.einsum("sgrh,kgh->grsk", rotary_queries, key_block, preferred_element_type=jnp.float32)
        * query_scale
    )
    capped = softcap_value * jnp.tanh(scores / softcap_value)
    if whole:
        allowed = (source >= 0) & (source < device_index)
        weights = jnp.where(allowed, jnp.exp(capped), 0.0)
    else:
        offsets = jnp.arange(rows, dtype=jnp.int32)
        query_pos = device_index * rows + offsets
        key_pos = source * rows + offsets
        distance = query_pos[:, None] - key_pos[None, :]
        allowed = (distance >= 0) & (distance < WINDOW_TOKENS) & (key_pos[None, :] >= 0)
        weights = jnp.where(allowed[None, None], jnp.exp(capped), 0.0)
    denominators = denominators + jnp.sum(weights, axis=-1)
    numerators = numerators + jnp.einsum(
        "grsk,kgh->grsh",
        weights.astype(jnp.bfloat16),
        value_block,
        preferred_element_type=jnp.float32,
    )
    return (numerators, denominators)


def along_lines(state, key_block, value_block, rotary_queries, device_index, cycle_size):
    kv_heads = key_block.shape[1]
    outer = cycle_size // 2
    def forward(step):
        return [(source, source + 2) for source in range(2 * step - 2, cycle_size - 2)]

    def across(step):
        pairs = [(2 * level, 2 * level + 1) for level in range(max(step - 1, 0), outer)]
        if step > 1:
            pairs = pairs + [(2 * level + 1, 2 * level) for level in range(step - 1, outer)]
        return pairs
    plane = device_index // 2
    side = device_index % 2

    rows = key_block.shape[0]
    whole = cycle_size * rows - 1 < WINDOW_TOKENS

    def attend_stacked(state, stacked, source):
        return attend_block(
            state, stacked[:, :kv_heads], stacked[:, kv_heads:], source, rotary_queries, device_index, whole
        )

    line = jnp.concatenate([key_block, value_block], axis=1)
    for step in range(1, outer + 1):
        last_forward = step == outer - 1
        if step == outer and outer >= 2:
            break
        if step < outer:
            arrived = lax.ppermute(line, "ctx", forward(step))
        crossed = lax.ppermute(line, "ctx", across(step))
        if last_forward:
            diagonal = lax.ppermute(
                line,
                "ctx",
                [(source, 2 * (source // 2) + 3 - source % 2) for source, unused in forward(step)],
            )
        state = attend_stacked(state, crossed, 2 * (plane - step + 1) + 1 - side)
        if step < outer:
            state = attend_stacked(state, arrived, device_index - 2 * step)
            line = arrived
        if last_forward:
            state = attend_stacked(state, diagonal, 2 * (plane - step) + 1 - side)
    return state


def exchanged(piece, count):
    pieces = [(piece, 0)]
    bit = count // 2
    while bit >= 1:
        pairs = [(source, source ^ bit) for source in range(count)]
        pieces = pieces + [(lax.ppermute(held, "tp", pairs), offset ^ bit) for held, offset in pieces]
        bit //= 2
    return pieces


def summed(partial, count):
    bit = 1
    while bit < count:
        partial = partial + lax.ppermute(partial, "tp", [(source, source ^ bit) for source in range(count)])
        bit *= 2
    return partial


def local(queries, keys, values, residual, out_weight, post_gain):
    rows = queries.shape[0]
    q_heads = queries.shape[1]
    head_size = queries.shape[2]
    kv_heads = keys.shape[1]
    heads_per_group = q_heads // kv_heads
    cycle_size = lax.axis_size("ctx")
    device_index = lax.axis_index("ctx")
    positions = (device_index * rows + jnp.arange(rows, dtype=jnp.int32))[:, None]
    rotary_queries = rotate(queries.astype(jnp.float32), positions).astype(jnp.bfloat16)
    rotary_queries = rotary_queries.reshape(rows, kv_heads, heads_per_group, head_size)
    rotary_keys = rotate(keys.astype(jnp.float32), positions).astype(jnp.bfloat16)
    reach = min((WINDOW_TOKENS + rows - 2) // rows, cycle_size - 1)
    state = (
        jnp.zeros((kv_heads, heads_per_group, rows, head_size), jnp.float32),
        jnp.zeros((kv_heads, heads_per_group, rows), jnp.float32),
    )
    state = attend_block(state, rotary_keys, values, device_index, rotary_queries, device_index)
    if reach == cycle_size - 1 and cycle_size % 2 == 0:
        state = along_lines(state, rotary_keys, values, rotary_queries, device_index, cycle_size)
    elif reach > 0:

        def advance(step_index, carried):
            running, key_block, value_block = carried
            key_block, value_block = passed_along((key_block, value_block), "ctx", 1)
            running = attend_block(
                running,
                key_block,
                value_block,
                device_index - step_index - 1,
                rotary_queries,
                device_index,
            )
            return (running, key_block, value_block)

        state, unused_keys, unused_values = lax.fori_loop(
            0, reach, advance, (state, rotary_keys, values)
        )
    numerators, denominators = state
    attended = (numerators / denominators[..., None]).astype(jnp.bfloat16)
    local_cols = out_weight.shape[2]
    tp_size = lax.axis_size("tp")
    tp_index = lax.axis_index("tp")
    butterfly = tp_size & (tp_size - 1) == 0
    if butterfly:
        projected = None
        for held, offset in exchanged(attended, tp_size):
            owner = jnp.bitwise_xor(tp_index, offset)
            weight_rows = lax.dynamic_slice_in_dim(out_weight, owner * q_heads, q_heads, 0)
            part = lax.dot_general(
                held,
                weight_rows.reshape(kv_heads, heads_per_group, head_size, local_cols),
                (((0, 1, 3), (0, 1, 2)), ((), ())),
                preferred_element_type=jnp.float32,
            )
            projected = part if projected is None else projected + part
    else:
        attended = jnp.transpose(attended, (2, 0, 1, 3)).reshape(rows, q_heads, head_size)
        piece = lax.all_gather(attended, "tp", axis=1, tiled=True)
        heads_in = piece.shape[1]
        weight_rows = out_weight.reshape(heads_in * head_size, local_cols)
        projected = jnp.dot(
            piece.reshape(rows, heads_in * head_size), weight_rows, preferred_element_type=jnp.float32
        )
    partial_sums = jnp.sum(projected * projected, axis=1)
    if butterfly:
        square_sums = summed(partial_sums, tp_size)
    else:
        square_sums = jnp.sum(lax.all_gather(partial_sums, "tp", axis=0), axis=0)
    normed = projected * lax.rsqrt(square_sums / D + 1e-06)[:, None] * post_gain.astype(jnp.float32)
    mixed = residual.astype(jnp.float32) + normed
    return mixed.astype(jnp.bfloat16)


def solution(mesh):
    in_specs = (
        P("ctx", "tp", None),
        P("ctx", "tp", None),
        P("ctx", "tp", None),
        P("ctx", "tp"),
        P(None, None, "tp"),
        P("tp"),
    )
    out_specs = P("ctx", "tp")
    return jax.shard_map(local, mesh=mesh, in_specs=in_specs, out_specs=out_specs, check_vma=False)
```

```python
import jax
import jax.numpy as jnp
from jax import lax
from jax.sharding import PartitionSpec as P

WINDOW_TOKENS = 4096
D = 3072


softcap_value = 50.0
query_scale = 1.0 / 12.0
rope_base = 10000.0


def passed_along(value, axis, steps):
    count = lax.axis_size(axis)
    first, last = (max(0, -steps), min(count, count - steps))
    return lax.ppermute(value, axis, [(source, source + steps) for source in range(first, last)])


def rotate(values_in, positions):
    half_width = values_in.shape[-1] // 2
    steps_half = jnp.arange(half_width, dtype=jnp.float32)
    inverse = rope_base ** (-2.0 * steps_half / values_in.shape[-1])
    angles = positions.astype(jnp.float32)[..., None] * inverse
    cosine = jnp.cos(angles)
    sine_part = jnp.sin(angles)
    first_half = values_in[..., :half_width]
    second_half = values_in[..., half_width:]
    return jnp.concatenate(
        [
            first_half * cosine - second_half * sine_part,
            second_half * cosine + first_half * sine_part,
        ],
        axis=-1,
    )


def attend_block(state, key_block, value_block, source, rotary_queries, device_index, whole=False):
    numerators, denominators = state
    rows = key_block.shape[0]
    scores = (
        jnp.einsum("sgrh,kgh->grsk", rotary_queries, key_block, preferred_element_type=jnp.float32)
        * query_scale
    )
    capped = softcap_value * jnp.tanh(scores / softcap_value)
    if whole:
        allowed = (source >= 0) & (source < device_index)
        weights = jnp.where(allowed, jnp.exp(capped), 0.0)
    else:
        offsets = jnp.arange(rows, dtype=jnp.int32)
        query_pos = device_index * rows + offsets
        key_pos = source * rows + offsets
        distance = query_pos[:, None] - key_pos[None, :]
        allowed = (distance >= 0) & (distance < WINDOW_TOKENS) & (key_pos[None, :] >= 0)
        weights = jnp.where(allowed[None, None], jnp.exp(capped), 0.0)
    denominators = denominators + jnp.sum(weights, axis=-1)
    numerators = numerators + jnp.einsum(
        "grsk,kgh->grsh",
        weights.astype(jnp.bfloat16),
        value_block,
        preferred_element_type=jnp.float32,
    )
    return (numerators, denominators)


def along_lines(state, key_block, value_block, rotary_queries, device_index, cycle_size):
    kv_heads = key_block.shape[1]
    outer = cycle_size // 2
    def forward(step):
        return [(source, source + 2) for source in range(2 * step - 2, cycle_size - 2)]

    def across(step):
        pairs = [(2 * level, 2 * level + 1) for level in range(max(step - 1, 0), outer)]
        if step > 1:
            pairs = pairs + [(2 * level + 1, 2 * level) for level in range(step - 1, outer)]
        return pairs
    plane = device_index // 2
    side = device_index % 2

    rows = key_block.shape[0]
    whole = cycle_size * rows - 1 < WINDOW_TOKENS

    def attend_stacked(state, stacked, source):
        return attend_block(
            state, stacked[:, :kv_heads], stacked[:, kv_heads:], source, rotary_queries, device_index, whole
        )

    line = jnp.concatenate([key_block, value_block], axis=1)
    for step in range(1, outer + 1):
        last_forward = step == outer - 1
        if step == outer and outer >= 2:
            break
        if step < outer:
            arrived = lax.ppermute(line, "ctx", forward(step))
        crossed = lax.ppermute(line, "ctx", across(step))
        if last_forward:
            diagonal = lax.ppermute(
                line,
                "ctx",
                [(source, 2 * (source // 2) + 3 - source % 2) for source, unused in forward(step)],
            )
        state = attend_stacked(state, crossed, 2 * (plane - step + 1) + 1 - side)
        if step < outer:
            state = attend_stacked(state, arrived, device_index - 2 * step)
            line = arrived
        if last_forward:
            state = attend_stacked(state, diagonal, 2 * (plane - step) + 1 - side)
    return state


def exchanged(piece, count):
    pieces = [(piece, 0)]
    bit = count // 2
    while bit >= 1:
        pairs = [(source, source ^ bit) for source in range(count)]
        pieces = pieces + [(lax.ppermute(held, "tp", pairs), offset ^ bit) for held, offset in pieces]
        bit //= 2
    return pieces


def summed(partial, count):
    total = partial
    for offset in range(1, count):
        total = total + lax.ppermute(partial, "tp", [(source, source ^ offset) for source in range(count)])
    return total


def local(queries, keys, values, residual, out_weight, post_gain):
    rows = queries.shape[0]
    q_heads = queries.shape[1]
    head_size = queries.shape[2]
    kv_heads = keys.shape[1]
    heads_per_group = q_heads // kv_heads
    cycle_size = lax.axis_size("ctx")
    device_index = lax.axis_index("ctx")
    positions = (device_index * rows + jnp.arange(rows, dtype=jnp.int32))[:, None]
    rotary_queries = rotate(queries.astype(jnp.float32), positions).astype(jnp.bfloat16)
    rotary_queries = rotary_queries.reshape(rows, kv_heads, heads_per_group, head_size)
    rotary_keys = rotate(keys.astype(jnp.float32), positions).astype(jnp.bfloat16)
    reach = min((WINDOW_TOKENS + rows - 2) // rows, cycle_size - 1)
    state = (
        jnp.zeros((kv_heads, heads_per_group, rows, head_size), jnp.float32),
        jnp.zeros((kv_heads, heads_per_group, rows), jnp.float32),
    )
    state = attend_block(state, rotary_keys, values, device_index, rotary_queries, device_index)
    if reach == cycle_size - 1 and cycle_size % 2 == 0:
        state = along_lines(state, rotary_keys, values, rotary_queries, device_index, cycle_size)
    elif reach > 0:

        def advance(step_index, carried):
            running, key_block, value_block = carried
            key_block, value_block = passed_along((key_block, value_block), "ctx", 1)
            running = attend_block(
                running,
                key_block,
                value_block,
                device_index - step_index - 1,
                rotary_queries,
                device_index,
            )
            return (running, key_block, value_block)

        state, unused_keys, unused_values = lax.fori_loop(
            0, reach, advance, (state, rotary_keys, values)
        )
    numerators, denominators = state
    attended = (numerators / denominators[..., None]).astype(jnp.bfloat16)
    local_cols = out_weight.shape[2]
    tp_size = lax.axis_size("tp")
    tp_index = lax.axis_index("tp")
    butterfly = tp_size & (tp_size - 1) == 0
    if butterfly:
        weight_sets = [out_weight]
        if tp_size >= 2:
            weight_sets.append(
                lax.ppermute(out_weight, "tp", [(source, source ^ 1) for source in range(tp_size)])
            )
        projections = [None] * len(weight_sets)
        for held, offset in exchanged(attended, tp_size):
            owner = jnp.bitwise_xor(tp_index, offset)
            for slot, weights in enumerate(weight_sets):
                weight_rows = lax.dynamic_slice_in_dim(weights, owner * q_heads, q_heads, 0)
                part = lax.dot_general(
                    held,
                    weight_rows.reshape(kv_heads, heads_per_group, head_size, local_cols),
                    (((0, 1, 3), (0, 1, 2)), ((), ())),
                    preferred_element_type=jnp.float32,
                )
                projections[slot] = part if projections[slot] is None else projections[slot] + part
        projected = projections[0]
    else:
        attended = jnp.transpose(attended, (2, 0, 1, 3)).reshape(rows, q_heads, head_size)
        piece = lax.all_gather(attended, "tp", axis=1, tiled=True)
        heads_in = piece.shape[1]
        weight_rows = out_weight.reshape(heads_in * head_size, local_cols)
        projected = jnp.dot(
            piece.reshape(rows, heads_in * head_size), weight_rows, preferred_element_type=jnp.float32
        )
    partial_sums = jnp.sum(projected * projected, axis=1)
    if butterfly:
        square_sums = partial_sums
        for extra in projections[1:]:
            square_sums = square_sums + jnp.sum(extra * extra, axis=1)
        bit = 2
        while bit < tp_size:
            square_sums = square_sums + lax.ppermute(
                square_sums, "tp", [(source, source ^ bit) for source in range(tp_size)]
            )
            bit *= 2
    else:
        square_sums = jnp.sum(lax.all_gather(partial_sums, "tp", axis=0), axis=0)
    normed = projected * lax.rsqrt(square_sums / D + 1e-06)[:, None] * post_gain.astype(jnp.float32)
    mixed = residual.astype(jnp.float32) + normed
    return mixed.astype(jnp.bfloat16)


def solution(mesh):
    in_specs = (
        P("ctx", "tp", None),
        P("ctx", "tp", None),
        P("ctx", "tp", None),
        P("ctx", "tp"),
        P(None, None, "tp"),
        P("tp"),
    )
    out_specs = P("ctx", "tp")
    return jax.shard_map(local, mesh=mesh, in_specs=in_specs, out_specs=out_specs, check_vma=False)
```

```python
import jax
import jax.numpy as jnp
from jax import lax
from jax.sharding import PartitionSpec as P

WINDOW_TOKENS = 4096
D = 3072


softcap_value = 50.0
query_scale = 1.0 / 12.0
rope_base = 10000.0


def passed_along(value, axis, steps):
    count = lax.axis_size(axis)
    first, last = (max(0, -steps), min(count, count - steps))
    return lax.ppermute(value, axis, [(source, source + steps) for source in range(first, last)])


def rotate(values_in, positions):
    half_width = values_in.shape[-1] // 2
    steps_half = jnp.arange(half_width, dtype=jnp.float32)
    inverse = rope_base ** (-2.0 * steps_half / values_in.shape[-1])
    angles = positions.astype(jnp.float32)[..., None] * inverse
    cosine = jnp.cos(angles)
    sine_part = jnp.sin(angles)
    first_half = values_in[..., :half_width]
    second_half = values_in[..., half_width:]
    return jnp.concatenate(
        [
            first_half * cosine - second_half * sine_part,
            second_half * cosine + first_half * sine_part,
        ],
        axis=-1,
    )


def attend_block(state, key_block, value_block, source, rotary_queries, device_index, whole=False):
    numerators, denominators = state
    rows = key_block.shape[0]
    scores = (
        jnp.einsum("sgrh,kgh->grsk", rotary_queries, key_block, preferred_element_type=jnp.float32)
        * query_scale
    )
    capped = softcap_value * jnp.tanh(scores / softcap_value)
    if whole:
        allowed = (source >= 0) & (source < device_index)
        weights = jnp.where(allowed, jnp.exp(capped), 0.0)
    else:
        offsets = jnp.arange(rows, dtype=jnp.int32)
        query_pos = device_index * rows + offsets
        key_pos = source * rows + offsets
        distance = query_pos[:, None] - key_pos[None, :]
        allowed = (distance >= 0) & (distance < WINDOW_TOKENS) & (key_pos[None, :] >= 0)
        weights = jnp.where(allowed[None, None], jnp.exp(capped), 0.0)
    denominators = denominators + jnp.sum(weights, axis=-1)
    numerators = numerators + jnp.einsum(
        "grsk,kgh->grsh",
        weights.astype(jnp.bfloat16),
        value_block,
        preferred_element_type=jnp.float32,
    )
    return (numerators, denominators)


def along_lines(state, key_block, value_block, rotary_queries, device_index, cycle_size):
    kv_heads = key_block.shape[1]
    outer = cycle_size // 2
    def forward(step):
        return [(source, source + 2) for source in range(2 * step - 2, cycle_size - 2)]

    def across(step):
        pairs = [(2 * level, 2 * level + 1) for level in range(max(step - 1, 0), outer)]
        if step > 1:
            pairs = pairs + [(2 * level + 1, 2 * level) for level in range(step - 1, outer)]
        return pairs
    plane = device_index // 2
    side = device_index % 2

    rows = key_block.shape[0]
    whole = cycle_size * rows - 1 < WINDOW_TOKENS

    def attend_stacked(state, stacked, source):
        return attend_block(
            state, stacked[:, :kv_heads], stacked[:, kv_heads:], source, rotary_queries, device_index, whole
        )

    line = jnp.concatenate([key_block, value_block], axis=1)
    for step in range(1, outer + 1):
        last_forward = step == outer - 1
        if step == outer and outer >= 2:
            break
        if step < outer:
            arrived = lax.ppermute(line, "ctx", forward(step))
        crossed = lax.ppermute(line, "ctx", across(step))
        if last_forward:
            diagonal = lax.ppermute(
                line,
                "ctx",
                [(source, 2 * (source // 2) + 3 - source % 2) for source, unused in forward(step)],
            )
        if step < outer:
            state = attend_stacked(state, arrived, device_index - 2 * step)
            line = arrived
        if last_forward:
            state = attend_stacked(state, diagonal, 2 * (plane - step) + 1 - side)
        state = attend_stacked(state, crossed, 2 * (plane - step + 1) + 1 - side)
    return state


def exchanged(piece, count):
    pieces = [(piece, 0)]
    bit = count // 2
    while bit >= 1:
        pairs = [(source, source ^ bit) for source in range(count)]
        pieces = pieces + [(lax.ppermute(held, "tp", pairs), offset ^ bit) for held, offset in pieces]
        bit //= 2
    return pieces


def summed(partial, count):
    total = partial
    for offset in range(1, count):
        total = total + lax.ppermute(partial, "tp", [(source, source ^ offset) for source in range(count)])
    return total


def local(queries, keys, values, residual, out_weight, post_gain):
    rows = queries.shape[0]
    q_heads = queries.shape[1]
    head_size = queries.shape[2]
    kv_heads = keys.shape[1]
    heads_per_group = q_heads // kv_heads
    cycle_size = lax.axis_size("ctx")
    device_index = lax.axis_index("ctx")
    positions = (device_index * rows + jnp.arange(rows, dtype=jnp.int32))[:, None]
    rotary_queries = rotate(queries.astype(jnp.float32), positions).astype(jnp.bfloat16)
    rotary_queries = rotary_queries.reshape(rows, kv_heads, heads_per_group, head_size)
    rotary_keys = rotate(keys.astype(jnp.float32), positions).astype(jnp.bfloat16)
    reach = min((WINDOW_TOKENS + rows - 2) // rows, cycle_size - 1)
    state = (
        jnp.zeros((kv_heads, heads_per_group, rows, head_size), jnp.float32),
        jnp.zeros((kv_heads, heads_per_group, rows), jnp.float32),
    )
    state = attend_block(state, rotary_keys, values, device_index, rotary_queries, device_index)
    if reach == cycle_size - 1 and cycle_size % 2 == 0:
        state = along_lines(state, rotary_keys, values, rotary_queries, device_index, cycle_size)
    elif reach > 0:

        def advance(step_index, carried):
            running, key_block, value_block = carried
            key_block, value_block = passed_along((key_block, value_block), "ctx", 1)
            running = attend_block(
                running,
                key_block,
                value_block,
                device_index - step_index - 1,
                rotary_queries,
                device_index,
            )
            return (running, key_block, value_block)

        state, unused_keys, unused_values = lax.fori_loop(
            0, reach, advance, (state, rotary_keys, values)
        )
    numerators, denominators = state
    attended = (numerators / denominators[..., None]).astype(jnp.bfloat16)
    local_cols = out_weight.shape[2]
    tp_size = lax.axis_size("tp")
    tp_index = lax.axis_index("tp")
    butterfly = tp_size & (tp_size - 1) == 0
    if butterfly:
        projected = None
        for held, offset in exchanged(attended, tp_size):
            owner = jnp.bitwise_xor(tp_index, offset)
            weight_rows = lax.dynamic_slice_in_dim(out_weight, owner * q_heads, q_heads, 0)
            part = lax.dot_general(
                held,
                weight_rows.reshape(kv_heads, heads_per_group, head_size, local_cols),
                (((0, 1, 3), (0, 1, 2)), ((), ())),
                preferred_element_type=jnp.float32,
            )
            projected = part if projected is None else projected + part
    else:
        attended = jnp.transpose(attended, (2, 0, 1, 3)).reshape(rows, q_heads, head_size)
        piece = lax.all_gather(attended, "tp", axis=1, tiled=True)
        heads_in = piece.shape[1]
        weight_rows = out_weight.reshape(heads_in * head_size, local_cols)
        projected = jnp.dot(
            piece.reshape(rows, heads_in * head_size), weight_rows, preferred_element_type=jnp.float32
        )
    partial_sums = jnp.sum(projected * projected, axis=1)
    if butterfly:
        square_sums = summed(partial_sums, tp_size)
    else:
        square_sums = jnp.sum(lax.all_gather(partial_sums, "tp", axis=0), axis=0)
    normed = projected * lax.rsqrt(square_sums / D + 1e-06)[:, None] * post_gain.astype(jnp.float32)
    mixed = residual.astype(jnp.float32) + normed
    return mixed.astype(jnp.bfloat16)


def solution(mesh):
    in_specs = (
        P("ctx", "tp", None),
        P("ctx", "tp", None),
        P("ctx", "tp", None),
        P("ctx", "tp"),
        P(None, None, "tp"),
        P("tp"),
    )
    out_specs = P("ctx", "tp")
    return jax.shard_map(local, mesh=mesh, in_specs=in_specs, out_specs=out_specs, check_vma=False)
```

```python
import jax
import jax.numpy as jnp
from jax import lax
from jax.sharding import PartitionSpec as P

WINDOW_TOKENS = 4096
D = 3072


softcap_value = 50.0
query_scale = 1.0 / 12.0
rope_base = 10000.0


def passed_along(value, axis, steps):
    count = lax.axis_size(axis)
    first, last = (max(0, -steps), min(count, count - steps))
    return lax.ppermute(value, axis, [(source, source + steps) for source in range(first, last)])


def rotate(values_in, positions):
    half_width = values_in.shape[-1] // 2
    steps_half = jnp.arange(half_width, dtype=jnp.float32)
    inverse = rope_base ** (-2.0 * steps_half / values_in.shape[-1])
    angles = positions.astype(jnp.float32)[..., None] * inverse
    cosine = jnp.cos(angles)
    sine_part = jnp.sin(angles)
    first_half = values_in[..., :half_width]
    second_half = values_in[..., half_width:]
    return jnp.concatenate(
        [
            first_half * cosine - second_half * sine_part,
            second_half * cosine + first_half * sine_part,
        ],
        axis=-1,
    )


def rotate_halves(values_in, positions):
    half_width = values_in.shape[-1] // 2
    steps_half = jnp.arange(half_width, dtype=jnp.float32)
    inverse = rope_base ** (-2.0 * steps_half / values_in.shape[-1])
    angles = positions.astype(jnp.float32)[..., None] * inverse
    cosine = jnp.cos(angles)
    sine_part = jnp.sin(angles)
    first_half = values_in[..., :half_width].astype(jnp.float32)
    second_half = values_in[..., half_width:].astype(jnp.float32)
    return jnp.concatenate(
        [
            first_half * cosine - second_half * sine_part,
            second_half * cosine + first_half * sine_part,
        ],
        axis=-1,
    )


def attend_block(state, key_block, value_block, source, rotary_queries, device_index, whole=False):
    numerators, denominators = state
    rows = key_block.shape[0]
    scores = (
        jnp.einsum("sgrh,kgh->grsk", rotary_queries, key_block, preferred_element_type=jnp.float32)
        * query_scale
    )
    capped = softcap_value * jnp.tanh(scores / softcap_value)
    if whole:
        allowed = (source >= 0) & (source < device_index)
        weights = jnp.where(allowed, jnp.exp(capped), 0.0)
    else:
        offsets = jnp.arange(rows, dtype=jnp.int32)
        query_pos = device_index * rows + offsets
        key_pos = source * rows + offsets
        distance = query_pos[:, None] - key_pos[None, :]
        allowed = (distance >= 0) & (distance < WINDOW_TOKENS) & (key_pos[None, :] >= 0)
        weights = jnp.where(allowed[None, None], jnp.exp(capped), 0.0)
    denominators = denominators + jnp.sum(weights, axis=-1)
    numerators = numerators + jnp.einsum(
        "grsk,kgh->grsh",
        weights.astype(jnp.bfloat16),
        value_block,
        preferred_element_type=jnp.float32,
    )
    return (numerators, denominators)


def along_lines(state, key_block, value_block, rotary_queries, device_index, cycle_size):
    kv_heads = key_block.shape[1]
    outer = cycle_size // 2
    def forward(step):
        return [(source, source + 2) for source in range(2 * step - 2, cycle_size - 2)]

    def across(step):
        pairs = [(2 * level, 2 * level + 1) for level in range(max(step - 1, 0), outer)]
        if step > 1:
            pairs = pairs + [(2 * level + 1, 2 * level) for level in range(step - 1, outer)]
        return pairs
    plane = device_index // 2
    side = device_index % 2

    rows = key_block.shape[0]
    whole = cycle_size * rows - 1 < WINDOW_TOKENS

    def attend_stacked(state, stacked, source):
        return attend_block(
            state, stacked[:, :kv_heads], stacked[:, kv_heads:], source, rotary_queries, device_index, whole
        )

    line = jnp.concatenate([key_block, value_block], axis=1)
    for step in range(1, outer + 1):
        last_forward = step == outer - 1
        if step == outer and outer >= 2:
            break
        if step < outer:
            arrived = lax.ppermute(line, "ctx", forward(step))
        crossed = lax.ppermute(line, "ctx", across(step))
        if last_forward:
            diagonal = lax.ppermute(
                line,
                "ctx",
                [(source, 2 * (source // 2) + 3 - source % 2) for source, unused in forward(step)],
            )
        state = attend_stacked(state, crossed, 2 * (plane - step + 1) + 1 - side)
        if step < outer:
            state = attend_stacked(state, arrived, device_index - 2 * step)
            line = arrived
        if last_forward:
            state = attend_stacked(state, diagonal, 2 * (plane - step) + 1 - side)
    return state


def exchanged(piece, count):
    pieces = [(piece, 0)]
    bit = count // 2
    while bit >= 1:
        pairs = [(source, source ^ bit) for source in range(count)]
        pieces = pieces + [(lax.ppermute(held, "tp", pairs), offset ^ bit) for held, offset in pieces]
        bit //= 2
    return pieces


def summed(partial, count):
    total = partial
    for offset in range(1, count):
        total = total + lax.ppermute(partial, "tp", [(source, source ^ offset) for source in range(count)])
    return total


def local(queries, keys, values, residual, out_weight, post_gain):
    rows = queries.shape[0]
    q_heads = queries.shape[1]
    head_size = queries.shape[2]
    kv_heads = keys.shape[1]
    heads_per_group = q_heads // kv_heads
    cycle_size = lax.axis_size("ctx")
    device_index = lax.axis_index("ctx")
    positions = (device_index * rows + jnp.arange(rows, dtype=jnp.int32))[:, None]
    rotary_queries = rotate(queries.astype(jnp.float32), positions).astype(jnp.bfloat16)
    rotary_queries = rotary_queries.reshape(rows, kv_heads, heads_per_group, head_size)
    rotary_keys = rotate_halves(keys, positions).astype(jnp.bfloat16)
    reach = min((WINDOW_TOKENS + rows - 2) // rows, cycle_size - 1)
    state = (
        jnp.zeros((kv_heads, heads_per_group, rows, head_size), jnp.float32),
        jnp.zeros((kv_heads, heads_per_group, rows), jnp.float32),
    )
    state = attend_block(state, rotary_keys, values, device_index, rotary_queries, device_index)
    if reach == cycle_size - 1 and cycle_size % 2 == 0:
        state = along_lines(state, rotary_keys, values, rotary_queries, device_index, cycle_size)
    elif reach > 0:

        def advance(step_index, carried):
            running, key_block, value_block = carried
            key_block, value_block = passed_along((key_block, value_block), "ctx", 1)
            running = attend_block(
                running,
                key_block,
                value_block,
                device_index - step_index - 1,
                rotary_queries,
                device_index,
            )
            return (running, key_block, value_block)

        state, unused_keys, unused_values = lax.fori_loop(
            0, reach, advance, (state, rotary_keys, values)
        )
    numerators, denominators = state
    attended = (numerators / denominators[..., None]).astype(jnp.bfloat16)
    local_cols = out_weight.shape[2]
    tp_size = lax.axis_size("tp")
    tp_index = lax.axis_index("tp")
    butterfly = tp_size & (tp_size - 1) == 0
    if butterfly:
        projected = None
        for held, offset in exchanged(attended, tp_size):
            owner = jnp.bitwise_xor(tp_index, offset)
            weight_rows = lax.dynamic_slice_in_dim(out_weight, owner * q_heads, q_heads, 0)
            part = lax.dot_general(
                held,
                weight_rows.reshape(kv_heads, heads_per_group, head_size, local_cols),
                (((0, 1, 3), (0, 1, 2)), ((), ())),
                preferred_element_type=jnp.float32,
            )
            projected = part if projected is None else projected + part
    else:
        attended = jnp.transpose(attended, (2, 0, 1, 3)).reshape(rows, q_heads, head_size)
        piece = lax.all_gather(attended, "tp", axis=1, tiled=True)
        heads_in = piece.shape[1]
        weight_rows = out_weight.reshape(heads_in * head_size, local_cols)
        projected = jnp.dot(
            piece.reshape(rows, heads_in * head_size), weight_rows, preferred_element_type=jnp.float32
        )
    partial_sums = jnp.sum(projected * projected, axis=1)
    if butterfly:
        square_sums = summed(partial_sums, tp_size)
    else:
        square_sums = jnp.sum(lax.all_gather(partial_sums, "tp", axis=0), axis=0)
    normed = projected * lax.rsqrt(square_sums / D + 1e-06)[:, None] * post_gain.astype(jnp.float32)
    mixed = residual.astype(jnp.float32) + normed
    return mixed.astype(jnp.bfloat16)


def solution(mesh):
    in_specs = (
        P("ctx", "tp", None),
        P("ctx", "tp", None),
        P("ctx", "tp", None),
        P("ctx", "tp"),
        P(None, None, "tp"),
        P("tp"),
    )
    out_specs = P("ctx", "tp")
    return jax.shard_map(local, mesh=mesh, in_specs=in_specs, out_specs=out_specs, check_vma=False)
```

```python
import jax
import jax.numpy as jnp
from jax import lax
from jax.sharding import PartitionSpec as P

WINDOW_TOKENS = 4096
D = 3072


softcap_value = 50.0
query_scale = 1.0 / 12.0
rope_base = 10000.0


def passed_along(value, axis, steps):
    count = lax.axis_size(axis)
    first, last = (max(0, -steps), min(count, count - steps))
    return lax.ppermute(value, axis, [(source, source + steps) for source in range(first, last)])


def rotate(values_in, positions):
    half_width = values_in.shape[-1] // 2
    steps_half = jnp.arange(half_width, dtype=jnp.float32)
    inverse = rope_base ** (-2.0 * steps_half / values_in.shape[-1])
    angles = positions.astype(jnp.float32)[..., None] * inverse
    cosine = jnp.cos(angles)
    sine_part = jnp.sin(angles)
    first_half = values_in[..., :half_width]
    second_half = values_in[..., half_width:]
    return jnp.concatenate(
        [
            first_half * cosine - second_half * sine_part,
            second_half * cosine + first_half * sine_part,
        ],
        axis=-1,
    )


def rotate_halves(values_in, positions):
    half_width = values_in.shape[-1] // 2
    steps_half = jnp.arange(half_width, dtype=jnp.float32)
    inverse = rope_base ** (-2.0 * steps_half / values_in.shape[-1])
    angles = positions.astype(jnp.float32)[..., None] * inverse
    cosine = jnp.cos(angles)
    sine_part = jnp.sin(angles)
    first_half = values_in[..., :half_width].astype(jnp.float32)
    second_half = values_in[..., half_width:].astype(jnp.float32)
    return jnp.concatenate(
        [
            first_half * cosine - second_half * sine_part,
            second_half * cosine + first_half * sine_part,
        ],
        axis=-1,
    )


def attend_block(state, key_block, value_block, source, rotary_queries, device_index, whole=False):
    numerators, denominators = state
    rows = key_block.shape[0]
    scores = (
        jnp.einsum("sgrh,kgh->grsk", rotary_queries, key_block, preferred_element_type=jnp.float32)
        * query_scale
    )
    capped = softcap_value * jnp.tanh(scores / softcap_value)
    if whole:
        allowed = (source >= 0) & (source < device_index)
        weights = jnp.where(allowed, jnp.exp(capped), 0.0)
    else:
        offsets = jnp.arange(rows, dtype=jnp.int32)
        query_pos = device_index * rows + offsets
        key_pos = source * rows + offsets
        distance = query_pos[:, None] - key_pos[None, :]
        allowed = (distance >= 0) & (distance < WINDOW_TOKENS) & (key_pos[None, :] >= 0)
        weights = jnp.where(allowed[None, None], jnp.exp(capped), 0.0)
    denominators = denominators + jnp.sum(weights, axis=-1)
    numerators = numerators + jnp.einsum(
        "grsk,kgh->grsh",
        weights.astype(jnp.bfloat16),
        value_block,
        preferred_element_type=jnp.float32,
    )
    return (numerators, denominators)


def along_lines(state, key_block, value_block, rotary_queries, device_index, cycle_size):
    kv_heads = key_block.shape[1]
    outer = cycle_size // 2
    def forward(step):
        return [(source, source + 2) for source in range(2 * step - 2, cycle_size - 2)]

    def across(step):
        pairs = [(2 * level, 2 * level + 1) for level in range(max(step - 1, 0), outer)]
        if step > 1:
            pairs = pairs + [(2 * level + 1, 2 * level) for level in range(step - 1, outer)]
        return pairs
    plane = device_index // 2
    side = device_index % 2

    rows = key_block.shape[0]
    whole = cycle_size * rows - 1 < WINDOW_TOKENS

    def attend_stacked(state, stacked, source):
        return attend_block(
            state, stacked[:, :kv_heads], stacked[:, kv_heads:], source, rotary_queries, device_index, whole
        )

    line = jnp.concatenate([key_block, value_block], axis=1)
    for step in range(1, outer + 1):
        last_forward = step == outer - 1
        if step == outer and outer >= 2:
            break
        if step < outer:
            arrived = lax.ppermute(line, "ctx", forward(step))
        crossed = lax.ppermute(line, "ctx", across(step))
        if last_forward:
            diagonal = lax.ppermute(
                line,
                "ctx",
                [(source, 2 * (source // 2) + 3 - source % 2) for source, unused in forward(step)],
            )
        state = attend_stacked(state, crossed, 2 * (plane - step + 1) + 1 - side)
        if step < outer:
            state = attend_stacked(state, arrived, device_index - 2 * step)
            line = arrived
        if last_forward:
            state = attend_stacked(state, diagonal, 2 * (plane - step) + 1 - side)
    return state


def exchanged(piece, count):
    pieces = [(piece, 0)]
    bit = count // 2
    while bit >= 1:
        pairs = [(source, source ^ bit) for source in range(count)]
        pieces = pieces + [(lax.ppermute(held, "tp", pairs), offset ^ bit) for held, offset in pieces]
        bit //= 2
    return pieces


def summed(partial, count):
    bit = 1
    while bit < count:
        partial = partial + lax.ppermute(partial, "tp", [(source, source ^ bit) for source in range(count)])
        bit *= 2
    return partial


def local(queries, keys, values, residual, out_weight, post_gain):
    rows = queries.shape[0]
    q_heads = queries.shape[1]
    head_size = queries.shape[2]
    kv_heads = keys.shape[1]
    heads_per_group = q_heads // kv_heads
    cycle_size = lax.axis_size("ctx")
    device_index = lax.axis_index("ctx")
    positions = (device_index * rows + jnp.arange(rows, dtype=jnp.int32))[:, None]
    rotary_queries = rotate(queries.astype(jnp.float32), positions).astype(jnp.bfloat16)
    rotary_queries = rotary_queries.reshape(rows, kv_heads, heads_per_group, head_size)
    rotary_keys = rotate_halves(keys, positions).astype(jnp.bfloat16)
    reach = min((WINDOW_TOKENS + rows - 2) // rows, cycle_size - 1)
    state = (
        jnp.zeros((kv_heads, heads_per_group, rows, head_size), jnp.float32),
        jnp.zeros((kv_heads, heads_per_group, rows), jnp.float32),
    )
    state = attend_block(state, rotary_keys, values, device_index, rotary_queries, device_index)
    if reach == cycle_size - 1 and cycle_size % 2 == 0:
        state = along_lines(state, rotary_keys, values, rotary_queries, device_index, cycle_size)
    elif reach > 0:

        def advance(step_index, carried):
            running, key_block, value_block = carried
            key_block, value_block = passed_along((key_block, value_block), "ctx", 1)
            running = attend_block(
                running,
                key_block,
                value_block,
                device_index - step_index - 1,
                rotary_queries,
                device_index,
            )
            return (running, key_block, value_block)

        state, unused_keys, unused_values = lax.fori_loop(
            0, reach, advance, (state, rotary_keys, values)
        )
    numerators, denominators = state
    attended = (numerators / denominators[..., None]).astype(jnp.bfloat16)
    local_cols = out_weight.shape[2]
    tp_size = lax.axis_size("tp")
    tp_index = lax.axis_index("tp")
    butterfly = tp_size & (tp_size - 1) == 0
    if butterfly:
        projected = None
        for held, offset in exchanged(attended, tp_size):
            owner = jnp.bitwise_xor(tp_index, offset)
            weight_rows = lax.dynamic_slice_in_dim(out_weight, owner * q_heads, q_heads, 0)
            part = lax.dot_general(
                held,
                weight_rows.reshape(kv_heads, heads_per_group, head_size, local_cols),
                (((0, 1, 3), (0, 1, 2)), ((), ())),
                preferred_element_type=jnp.float32,
            )
            projected = part if projected is None else projected + part
    else:
        attended = jnp.transpose(attended, (2, 0, 1, 3)).reshape(rows, q_heads, head_size)
        piece = lax.all_gather(attended, "tp", axis=1, tiled=True)
        heads_in = piece.shape[1]
        weight_rows = out_weight.reshape(heads_in * head_size, local_cols)
        projected = jnp.dot(
            piece.reshape(rows, heads_in * head_size), weight_rows, preferred_element_type=jnp.float32
        )
    partial_sums = jnp.sum(projected * projected, axis=1)
    if butterfly:
        square_sums = summed(partial_sums, tp_size)
    else:
        square_sums = jnp.sum(lax.all_gather(partial_sums, "tp", axis=0), axis=0)
    normed = projected * lax.rsqrt(square_sums / D + 1e-06)[:, None] * post_gain.astype(jnp.float32)
    mixed = residual.astype(jnp.float32) + normed
    return mixed.astype(jnp.bfloat16)


def solution(mesh):
    in_specs = (
        P("ctx", "tp", None),
        P("ctx", "tp", None),
        P("ctx", "tp", None),
        P("ctx", "tp"),
        P(None, None, "tp"),
        P("tp"),
    )
    out_specs = P("ctx", "tp")
    return jax.shard_map(local, mesh=mesh, in_specs=in_specs, out_specs=out_specs, check_vma=False)
```
